512 devices in a mesh: grp: 4 (over y), walk: 128 (over x, z, core).
Axes of the slice: x: 4, y: 4, z: 16, core: 2. Of those that a mesh axis runs over, the one named last changes fastest.
Arguments:
- log_grads: float32 [1024, 131072], P('walk', 'grp'), may hold values from -60 to 60, as said below
- energies: float32 [1024], P('walk'), may hold values from -6 to 6
Outputs:
- update: float32 [131072], P(('grp', 'walk'))
The draws below stay inside these ranges and needn't reach their ends.
Inputs may be any that keep to these rules, and one draw needn't show every extreme that they name: `log_grads`: real-valued gradients, every row and column with its own scale.
All inputs are finite; a program needn't handle non-finite values.
Results may differ from the reference program's by a relative error of at most 0.0003.
Values sent between devices are 32-bit elements; how exact they have to be, the bound alone decides.
No kernel may reach another device: no remote copies, remote signals or barrier semaphores. Data moves between devices by JAX's collectives and lax.ppermute only.
A program may use at most 128 MiB of HBM per device.

```python
import jax
import jax.numpy as jnp
from jax import lax

WALKERS = 1024
PARAMS = 131072


def draw_log_grads(key, part):
    keys = jax.random.split(jax.random.fold_in(key, 17), 4)
    base = jax.random.truncated_normal(keys[0], -6.0, 6.0, (WALKERS, PARAMS), jnp.float32)
    ramp = jnp.exp((jnp.arange(PARAMS, dtype=jnp.float32) / PARAMS - 0.5) * jnp.log(3.0))
    column_scale = jnp.exp(jax.random.uniform(keys[1], (PARAMS,), jnp.float32, jnp.log(0.3), jnp.log(3.0))) * ramp
    row_scale = jnp.exp(jax.random.uniform(keys[2], (WALKERS, 1), jnp.float32, jnp.log(0.3), jnp.log(3.0)))
    offset = jax.random.truncated_normal(keys[3], -4.0, 4.0, (PARAMS,), jnp.float32)
    values = base * row_scale * column_scale + offset * column_scale
    return jnp.clip(values, -60.0, 60.0)


def level_of(key, extent, cuts, low, top_value):
    def one(position, parts):
        steps = jax.random.uniform(jax.random.fold_in(jax.random.fold_in(key, 6), position), (parts,), jnp.float32, low / len(cuts), top_value / len(cuts))
        return jnp.repeat(jnp.exp(steps), extent[position] // parts).reshape((-1,) + (1,) * (len(extent) - position - 1))

    factor_of = one(*cuts[0])
    for cut in cuts[1:]:
        factor_of = factor_of * one(*cut)
    return factor_of


def normal_values(rng, extent, spread, reach, shards=(), kind=jnp.bfloat16):
    array = jax.random.normal(rng, extent, jnp.float32) * spread
    if len(shards) > 0:
        array = level_of(rng, extent, shards, -0.22, 0.18) * array
    return jnp.clip(array, min=-reach, max=reach).astype(kind)


def setup_inputs(seed: int = 0) -> dict:
    key_list = jax.random.split(jax.random.key(seed), 3)
    log_grads = draw_log_grads(jax.random.fold_in(key_list[2], 71), 0)
    energies = normal_values(key_list[1], (WALKERS,), 1.0, 6.0, ((0, 128),), jnp.float32)
    return {"log_grads": log_grads, "energies": energies}


damping = 0.0004

def reference(log_grads, energies):
    column_mean = lax.optimization_barrier(jnp.mean(log_grads, axis=0, keepdims=True))
    centred = (log_grads - column_mean) / jnp.sqrt(jnp.float32(WALKERS))
    scaled_energy = (energies - jnp.mean(energies)) / jnp.sqrt(jnp.float32(WALKERS))
    gram = jnp.dot(centred, centred.T, precision=lax.Precision.HIGHEST)
    system = gram + damping * PARAMS * jnp.eye(WALKERS, dtype=jnp.float32)
    solved = jnp.linalg.solve(system, scaled_energy)
    update = jnp.dot(solved, centred, precision=lax.Precision.HIGHEST)
    return -(PARAMS / jnp.sqrt(jnp.float32(WALKERS))) * update
```

```python
import jax
import jax.numpy as jnp
import numpy as np
from jax import lax
from jax.sharding import Mesh
from jax.sharding import PartitionSpec as P

WALKERS = 1024
BLOCK = 128


damping = 0.0004

WALK_PARTS = ("wx", "wz", "wc")


def split_walk(walk):
    if walk % 32 == 0 and walk // 32 <= 4:
        return (walk // 32, 16, 2)
    return (1, 1, walk)


def factor_solve(factor, rhs):
    column = rhs[:, None]
    first = lax.linalg.triangular_solve(factor, column, left_side=True, lower=True)
    second = lax.linalg.triangular_solve(
        factor, first, left_side=True, lower=True, transpose_a=True
    )
    return second[:, 0]


def reduce_scatter(x, levels):
    for axis, size in levels:
        rows = x.shape[0]
        parts = x.reshape(size, rows // size, x.shape[1])
        x = lax.all_to_all(parts, axis, 0, 0, tiled=True).sum(0)
    return x


def all_gather(x, levels):
    for axis, size in levels:
        copies = jnp.broadcast_to(x[None], (size,) + x.shape)
        x = lax.all_to_all(copies, axis, 0, 0, tiled=True)
    return x


def upper_pairs(nb):
    return [(i, j) for i in range(nb) for j in range(i, nb)]


def pack_upper(gram, nb):
    blocks = gram.reshape(nb, BLOCK, nb, BLOCK)
    return jnp.stack([blocks[i, :, j, :] for i, j in upper_pairs(nb)])


def unpack_upper(packed, nb):
    where = {pair: k for k, pair in enumerate(upper_pairs(nb))}
    rows = []
    for i in range(nb):
        row = []
        for j in range(nb):
            if i <= j:
                row.append(packed[where[(i, j)]])
            else:
                row.append(packed[where[(j, i)]].T)
        rows.append(jnp.concatenate(row, axis=1))
    return jnp.concatenate(rows, axis=0)


def make_on_device(sizes):
    grp, wx, wz, wc = sizes
    levels = [("grp", grp), ("wc", wc), ("wx", wx), ("wz", wz)]
    levels = [(a, n) for a, n in levels if n > 1]
    n_dev = grp * wx * wz * wc

    def on_device(log_grads, energies):
        walk_axes = WALK_PARTS
        regrouped = lax.all_to_all(
            log_grads, walk_axes, split_axis=1, concat_axis=0, tiled=True
        )
        walk = wx * wz * wc
        group_params = regrouped.shape[1] * walk
        total_params = group_params * grp
        root_walkers = jnp.sqrt(jnp.float32(WALKERS))
        column_mean = jnp.mean(regrouped, axis=0, keepdims=True)
        centred = (regrouped - column_mean) / root_walkers
        local_gram = jnp.dot(centred, centred.T, precision=lax.Precision.HIGHEST)

        nb = WALKERS // BLOCK
        packed = pack_upper(local_gram, nb)
        n_blocks = packed.shape[0]
        flat = packed.reshape(n_blocks * BLOCK, BLOCK)
        chunk = reduce_scatter(flat, levels)
        per_dev = chunk.shape[0]
        energy_row = jnp.zeros((1, BLOCK), jnp.float32)
        energy_row = energy_row.at[0, : energies.shape[0]].set(energies)
        chunk = jnp.concatenate([chunk, energy_row], axis=0)
        gathered = all_gather(chunk, levels[::-1])
        gathered = gathered.reshape(grp, wc, wx, wz, per_dev + 1, BLOCK)
        whole_packed = gathered[..., :per_dev, :].reshape(n_blocks, BLOCK, BLOCK)
        per_walk = energies.shape[0]
        all_energy = gathered[0, :, :, :, per_dev, :per_walk]
        all_energy = jnp.transpose(all_energy, (1, 2, 0, 3)).reshape(WALKERS)

        whole_gram = unpack_upper(whole_packed, nb)
        scaled_energy = (all_energy - jnp.mean(all_energy)) / root_walkers
        identity_mat = jnp.eye(WALKERS, dtype=jnp.float32)
        factor = jnp.linalg.cholesky(whole_gram + damping * total_params * identity_mat)
        solved = factor_solve(factor, scaled_energy)
        update = jnp.dot(solved, centred, precision=lax.Precision.HIGHEST)
        return -(total_params / root_walkers) * update

    return on_device


def solution(mesh):
    grp = mesh.shape["grp"]
    walk = mesh.shape["walk"]
    wx, wz, wc = split_walk(walk)
    devices = np.asarray(mesh.devices).reshape(grp, wx, wz, wc)
    fine = Mesh(devices, ("grp",) + WALK_PARTS)
    return jax.shard_map(
        make_on_device((grp, wx, wz, wc)),
        mesh=fine,
        in_specs=(P(WALK_PARTS, "grp"), P(WALK_PARTS)),
        out_specs=P(("grp",) + WALK_PARTS),
        check_vma=False,
    )
```

```python
import jax
import jax.numpy as jnp
import numpy as np
from jax import lax
from jax.sharding import Mesh
from jax.sharding import PartitionSpec as P

WALKERS = 1024
BLOCK = 128


damping = 0.0004

WALK_PARTS = ("wx", "wz", "wc")


def split_walk(walk):
    if walk % 32 == 0 and walk // 32 <= 4:
        return (walk // 32, 16, 2)
    return (1, 1, walk)


def factor_solve(factor, rhs):
    column = rhs[:, None]
    first = lax.linalg.triangular_solve(factor, column, left_side=True, lower=True)
    second = lax.linalg.triangular_solve(
        factor, first, left_side=True, lower=True, transpose_a=True
    )
    return second[:, 0]


def reduce_scatter(x, levels):
    for axis, size in levels:
        rows = x.shape[0]
        parts = x.reshape(size, rows // size, x.shape[1])
        x = lax.all_to_all(parts, axis, 0, 0, tiled=True).sum(0)
    return x


def all_gather(x, levels):
    for axis, size in levels:
        copies = jnp.broadcast_to(x[None], (size,) + x.shape)
        x = lax.all_to_all(copies, axis, 0, 0, tiled=True)
    return x


def upper_pairs(nb):
    return [(i, j) for i in range(nb) for j in range(i, nb)]


def pack_upper(gram, nb):
    blocks = gram.reshape(nb, BLOCK, nb, BLOCK)
    return jnp.stack([blocks[i, :, j, :] for i, j in upper_pairs(nb)])


def unpack_upper(packed, nb):
    where = {pair: k for k, pair in enumerate(upper_pairs(nb))}
    index = np.array(
        [[where[(min(i, j), max(i, j))] for j in range(nb)] for i in range(nb)]
    )
    blocks = packed[index.reshape(-1)].reshape(nb, nb, BLOCK, BLOCK)
    below = np.arange(nb)[:, None] > np.arange(nb)[None, :]
    blocks = jnp.where(below[:, :, None, None], jnp.swapaxes(blocks, 2, 3), blocks)
    return jnp.transpose(blocks, (0, 2, 1, 3)).reshape(nb * BLOCK, nb * BLOCK)


def cholesky_solve(system, rhs, nb):
    hi = lax.Precision.HIGHEST
    eye = jnp.eye(BLOCK, dtype=jnp.float32)
    inverses, panels, partial = [], [], []
    for k in range(nb):
        lo, up = k * BLOCK, (k + 1) * BLOCK
        factor = lax.linalg.cholesky(system[lo:up, lo:up], symmetrize_input=False)
        inverse = lax.linalg.triangular_solve(factor, eye, left_side=True, lower=True)
        part = jnp.dot(inverse, rhs[lo:up], precision=hi)
        inverses.append(inverse)
        partial.append(part)
        if k + 1 < nb:
            panel = jnp.dot(system[up:, lo:up], inverse.T, precision=hi)
            panels.append(panel)
            trailing = system[up:, up:] - jnp.dot(panel, panel.T, precision=hi)
            system = system.at[up:, up:].set(trailing)
            rhs = rhs.at[up:].add(-jnp.dot(panel, part, precision=hi))
    solved = [None] * nb
    tail = None
    for k in reversed(range(nb)):
        value = partial[k]
        if tail is not None:
            value = value - jnp.dot(tail, panels[k], precision=hi)
        solved[k] = jnp.dot(value, inverses[k], precision=hi)
        tail = solved[k] if tail is None else jnp.concatenate([solved[k], tail])
    return jnp.concatenate(solved)


def make_on_device(sizes):
    grp, wx, wz, wc = sizes
    levels = [("grp", grp), ("wc", wc), ("wx", wx), ("wz", wz)]
    levels = [(a, n) for a, n in levels if n > 1]
    n_dev = grp * wx * wz * wc

    def on_device(log_grads, energies):
        walk_axes = WALK_PARTS
        regrouped = lax.all_to_all(
            log_grads, walk_axes, split_axis=1, concat_axis=0, tiled=True
        )
        walk = wx * wz * wc
        group_params = regrouped.shape[1] * walk
        total_params = group_params * grp
        root_walkers = jnp.sqrt(jnp.float32(WALKERS))
        column_mean = jnp.mean(regrouped, axis=0, keepdims=True)
        centred = (regrouped - column_mean) / root_walkers
        local_gram = jnp.dot(centred, centred.T, precision=lax.Precision.HIGHEST)

        nb = WALKERS // BLOCK
        packed = pack_upper(local_gram, nb)
        n_blocks = packed.shape[0]
        flat = packed.reshape(n_blocks * BLOCK, BLOCK)
        chunk = reduce_scatter(flat, levels)
        per_dev = chunk.shape[0]
        energy_row = jnp.zeros((1, BLOCK), jnp.float32)
        energy_row = energy_row.at[0, : energies.shape[0]].set(energies)
        chunk = jnp.concatenate([chunk, energy_row], axis=0)
        gathered = all_gather(chunk, levels[::-1])
        gathered = gathered.reshape(grp, wc, wx, wz, per_dev + 1, BLOCK)
        whole_packed = gathered[..., :per_dev, :].reshape(n_blocks, BLOCK, BLOCK)
        per_walk = energies.shape[0]
        all_energy = gathered[0, :, :, :, per_dev, :per_walk]
        all_energy = jnp.transpose(all_energy, (1, 2, 0, 3)).reshape(WALKERS)

        whole_gram = unpack_upper(whole_packed, nb)
        scaled_energy = (all_energy - jnp.mean(all_energy)) / root_walkers
        identity_mat = jnp.eye(WALKERS, dtype=jnp.float32)
        system = whole_gram + damping * total_params * identity_mat
        solved = cholesky_solve(system, scaled_energy, nb)
        update = jnp.dot(solved, centred, precision=lax.Precision.HIGHEST)
        return -(total_params / root_walkers) * update

    return on_device


def solution(mesh):
    grp = mesh.shape["grp"]
    walk = mesh.shape["walk"]
    wx, wz, wc = split_walk(walk)
    devices = np.asarray(mesh.devices).reshape(grp, wx, wz, wc)
    fine = Mesh(devices, ("grp",) + WALK_PARTS)
    return jax.shard_map(
        make_on_device((grp, wx, wz, wc)),
        mesh=fine,
        in_specs=(P(WALK_PARTS, "grp"), P(WALK_PARTS)),
        out_specs=P(("grp",) + WALK_PARTS),
        check_vma=False,
    )
```

```python
import jax
import jax.numpy as jnp
import numpy as np
from jax import lax
from jax.sharding import Mesh
from jax.sharding import PartitionSpec as P

WALKERS = 1024
BLOCK = 128
CG_STEPS = 12
CG_TOL = 2e-5


damping = 0.0004

WALK_PARTS = ("wx", "wz", "wc")


def split_walk(walk):
    if walk % 32 == 0 and walk // 32 <= 4:
        return (walk // 32, 16, 2)
    return (1, 1, walk)


def factor_solve(factor, rhs):
    column = rhs[:, None]
    first = lax.linalg.triangular_solve(factor, column, left_side=True, lower=True)
    second = lax.linalg.triangular_solve(
        factor, first, left_side=True, lower=True, transpose_a=True
    )
    return second[:, 0]


def reduce_scatter(x, levels):
    for axis, size in levels:
        rows = x.shape[0]
        parts = x.reshape(size, rows // size, x.shape[1])
        x = lax.all_to_all(parts, axis, 0, 0, tiled=True).sum(0)
    return x


def all_gather(x, levels):
    for axis, size in levels:
        copies = jnp.broadcast_to(x[None], (size,) + x.shape)
        x = lax.all_to_all(copies, axis, 0, 0, tiled=True)
    return x


def upper_pairs(nb):
    return [(i, j) for i in range(nb) for j in range(i, nb)]


def pack_upper(gram, nb):
    blocks = gram.reshape(nb, BLOCK, nb, BLOCK)
    return jnp.stack([blocks[i, :, j, :] for i, j in upper_pairs(nb)])


def unpack_upper(packed, nb):
    where = {pair: k for k, pair in enumerate(upper_pairs(nb))}
    index = np.array(
        [[where[(min(i, j), max(i, j))] for j in range(nb)] for i in range(nb)]
    )
    blocks = packed[index.reshape(-1)].reshape(nb, nb, BLOCK, BLOCK)
    below = np.arange(nb)[:, None] > np.arange(nb)[None, :]
    blocks = jnp.where(below[:, :, None, None], jnp.swapaxes(blocks, 2, 3), blocks)
    return jnp.transpose(blocks, (0, 2, 1, 3)).reshape(nb * BLOCK, nb * BLOCK)


def cholesky_solve(system, rhs, nb):
    hi = lax.Precision.HIGHEST
    eye = jnp.eye(BLOCK, dtype=jnp.float32)
    inverses, panels, partial = [], [], []
    for k in range(nb):
        lo, up = k * BLOCK, (k + 1) * BLOCK
        factor = lax.linalg.cholesky(system[lo:up, lo:up], symmetrize_input=False)
        inverse = lax.linalg.triangular_solve(factor, eye, left_side=True, lower=True)
        part = jnp.dot(inverse, rhs[lo:up], precision=hi)
        inverses.append(inverse)
        partial.append(part)
        if k + 1 < nb:
            panel = jnp.dot(system[up:, lo:up], inverse.T, precision=hi)
            panels.append(panel)
            trailing = system[up:, up:] - jnp.dot(panel, panel.T, precision=hi)
            system = system.at[up:, up:].set(trailing)
            rhs = rhs.at[up:].add(-jnp.dot(panel, part, precision=hi))
    solved = [None] * nb
    tail = None
    for k in reversed(range(nb)):
        value = partial[k]
        if tail is not None:
            value = value - jnp.dot(tail, panels[k], precision=hi)
        solved[k] = jnp.dot(value, inverses[k], precision=hi)
        tail = solved[k] if tail is None else jnp.concatenate([solved[k], tail])
    return jnp.concatenate(solved)


def certified_cg(system, rhs, lam, steps, tol):
    hi = lax.Precision.HIGHEST
    inv_diag = 1.0 / jnp.diagonal(system)
    x = jnp.zeros_like(rhs)
    r = rhs
    z = r * inv_diag
    p = z
    rz = jnp.dot(r, z, precision=hi)
    for _ in range(steps):
        ap = jnp.dot(system, p, precision=hi)
        alpha = rz / jnp.dot(p, ap, precision=hi)
        x = x + alpha * p
        r = r - alpha * ap
        z = r * inv_diag
        rz_next = jnp.dot(r, z, precision=hi)
        p = z + (rz_next / rz) * p
        rz = rz_next
    ax = jnp.dot(system, x, precision=hi)
    resid = rhs - ax
    energy = jnp.dot(x, ax, precision=hi) - lam * jnp.dot(x, x, precision=hi)
    bound = jnp.dot(resid, resid, precision=hi)
    ok = bound <= (tol * tol) * lam * energy
    return x, ok


def make_on_device(sizes):
    grp, wx, wz, wc = sizes
    levels = [("grp", grp), ("wc", wc), ("wx", wx), ("wz", wz)]
    levels = [(a, n) for a, n in levels if n > 1]
    n_dev = grp * wx * wz * wc

    def on_device(log_grads, energies):
        walk_axes = WALK_PARTS
        regrouped = lax.all_to_all(
            log_grads, walk_axes, split_axis=1, concat_axis=0, tiled=True
        )
        walk = wx * wz * wc
        group_params = regrouped.shape[1] * walk
        total_params = group_params * grp
        root_walkers = jnp.sqrt(jnp.float32(WALKERS))
        column_mean = jnp.mean(regrouped, axis=0, keepdims=True)
        centred = (regrouped - column_mean) / root_walkers
        local_gram = jnp.dot(centred, centred.T, precision=lax.Precision.HIGHEST)

        nb = WALKERS // BLOCK
        packed = pack_upper(local_gram, nb)
        n_blocks = packed.shape[0]
        flat = packed.reshape(n_blocks * BLOCK, BLOCK)
        chunk = reduce_scatter(flat, levels)
        per_dev = chunk.shape[0]
        energy_row = jnp.zeros((1, BLOCK), jnp.float32)
        energy_row = energy_row.at[0, : energies.shape[0]].set(energies)
        chunk = jnp.concatenate([chunk, energy_row], axis=0)
        gathered = all_gather(chunk, levels[::-1])
        gathered = gathered.reshape(grp, wc, wx, wz, per_dev + 1, BLOCK)
        whole_packed = gathered[..., :per_dev, :].reshape(n_blocks, BLOCK, BLOCK)
        per_walk = energies.shape[0]
        all_energy = gathered[0, :, :, :, per_dev, :per_walk]
        all_energy = jnp.transpose(all_energy, (1, 2, 0, 3)).reshape(WALKERS)

        whole_gram = unpack_upper(whole_packed, nb)
        scaled_energy = (all_energy - jnp.mean(all_energy)) / root_walkers
        identity_mat = jnp.eye(WALKERS, dtype=jnp.float32)
        lam = damping * total_params
        system = whole_gram + lam * identity_mat
        guess, ok = certified_cg(system, scaled_energy, lam, CG_STEPS, CG_TOL)
        solved = lax.cond(
            ok,
            lambda a, b, g: g,
            lambda a, b, g: cholesky_solve(a, b, nb),
            system,
            scaled_energy,
            guess,
        )
        update = jnp.dot(solved, centred, precision=lax.Precision.HIGHEST)
        return -(total_params / root_walkers) * update

    return on_device


def solution(mesh):
    grp = mesh.shape["grp"]
    walk = mesh.shape["walk"]
    wx, wz, wc = split_walk(walk)
    devices = np.asarray(mesh.devices).reshape(grp, wx, wz, wc)
    fine = Mesh(devices, ("grp",) + WALK_PARTS)
    return jax.shard_map(
        make_on_device((grp, wx, wz, wc)),
        mesh=fine,
        in_specs=(P(WALK_PARTS, "grp"), P(WALK_PARTS)),
        out_specs=P(("grp",) + WALK_PARTS),
        check_vma=False,
    )
```

```python
import jax
import jax.numpy as jnp
import numpy as np
from jax import lax
from jax.sharding import Mesh
from jax.sharding import PartitionSpec as P

WALKERS = 1024
BLOCK = 128
CG_STEPS = 12
CG_TOL = 2e-5


damping = 0.0004

WALK_PARTS = ("wx", "wz", "wc")


def split_walk(walk):
    if walk % 32 == 0 and walk // 32 <= 4:
        return (walk // 32, 16, 2)
    return (1, 1, walk)


def factor_solve(factor, rhs):
    column = rhs[:, None]
    first = lax.linalg.triangular_solve(factor, column, left_side=True, lower=True)
    second = lax.linalg.triangular_solve(
        factor, first, left_side=True, lower=True, transpose_a=True
    )
    return second[:, 0]


def reduce_scatter(x, levels):
    for axis, size in levels:
        rows = x.shape[0]
        parts = x.reshape(size, rows // size, x.shape[1])
        x = lax.all_to_all(parts, axis, 0, 0, tiled=True).sum(0)
    return x


def all_gather(x, levels):
    for axis, size in levels:
        copies = jnp.broadcast_to(x[None], (size,) + x.shape)
        x = lax.all_to_all(copies, axis, 0, 0, tiled=True)
    return x


def upper_pairs(nb):
    return [(i, j) for i in range(nb) for j in range(i, nb)]


def pack_upper(gram, nb):
    blocks = gram.reshape(nb, BLOCK, nb, BLOCK)
    return jnp.stack([blocks[i, :, j, :] for i, j in upper_pairs(nb)])


def unpack_upper(packed, nb):
    where = {pair: k for k, pair in enumerate(upper_pairs(nb))}
    index = np.array(
        [[where[(min(i, j), max(i, j))] for j in range(nb)] for i in range(nb)]
    )
    blocks = packed[index.reshape(-1)].reshape(nb, nb, BLOCK, BLOCK)
    below = np.arange(nb)[:, None] > np.arange(nb)[None, :]
    inner = np.arange(BLOCK)[:, None] > np.arange(BLOCK)[None, :]
    diag = np.eye(nb, dtype=bool)
    mirror = below[:, :, None, None] | (diag[:, :, None, None] & inner[None, None])
    blocks = jnp.where(mirror, jnp.swapaxes(blocks, 2, 3), blocks)
    return jnp.transpose(blocks, (0, 2, 1, 3)).reshape(nb * BLOCK, nb * BLOCK)


def cholesky_solve(system, rhs, nb):
    hi = lax.Precision.HIGHEST
    eye = jnp.eye(BLOCK, dtype=jnp.float32)
    inverses, panels, partial = [], [], []
    for k in range(nb):
        lo, up = k * BLOCK, (k + 1) * BLOCK
        factor = lax.linalg.cholesky(system[lo:up, lo:up], symmetrize_input=False)
        inverse = lax.linalg.triangular_solve(factor, eye, left_side=True, lower=True)
        part = jnp.dot(inverse, rhs[lo:up], precision=hi)
        inverses.append(inverse)
        partial.append(part)
        if k + 1 < nb:
            panel = jnp.dot(system[up:, lo:up], inverse.T, precision=hi)
            panels.append(panel)
            trailing = system[up:, up:] - jnp.dot(panel, panel.T, precision=hi)
            system = system.at[up:, up:].set(trailing)
            rhs = rhs.at[up:].add(-jnp.dot(panel, part, precision=hi))
    solved = [None] * nb
    tail = None
    for k in reversed(range(nb)):
        value = partial[k]
        if tail is not None:
            value = value - jnp.dot(tail, panels[k], precision=hi)
        solved[k] = jnp.dot(value, inverses[k], precision=hi)
        tail = solved[k] if tail is None else jnp.concatenate([solved[k], tail])
    return jnp.concatenate(solved)


def sym_matvec(system, v):
    return jnp.sum(system * v[:, None], axis=0)


def certified_cg(system, rhs, lam, steps, tol):
    hi = lax.Precision.HIGHEST
    eye = np.eye(system.shape[0], dtype=bool)
    inv_diag = 1.0 / jnp.sum(jnp.where(eye, system, 0.0), axis=0)
    x = jnp.zeros_like(rhs)
    r = rhs
    z = r * inv_diag
    p = z
    rz = jnp.dot(r, z, precision=hi)
    for _ in range(steps):
        ap = sym_matvec(system, p)
        alpha = rz / jnp.dot(p, ap, precision=hi)
        x = x + alpha * p
        r = r - alpha * ap
        z = r * inv_diag
        rz_next = jnp.dot(r, z, precision=hi)
        p = z + (rz_next / rz) * p
        rz = rz_next
    ax = sym_matvec(system, x)
    resid = rhs - ax
    energy = jnp.dot(x, ax, precision=hi) - lam * jnp.dot(x, x, precision=hi)
    bound = jnp.dot(resid, resid, precision=hi)
    ok = bound <= (tol * tol) * lam * energy
    return x, ok


def make_on_device(sizes):
    grp, wx, wz, wc = sizes
    levels = [("grp", grp), ("wc", wc), ("wx", wx), ("wz", wz)]
    levels = [(a, n) for a, n in levels if n > 1]
    n_dev = grp * wx * wz * wc

    def on_device(log_grads, energies):
        walk_axes = WALK_PARTS
        regrouped = lax.all_to_all(
            log_grads, walk_axes, split_axis=1, concat_axis=0, tiled=True
        )
        walk = wx * wz * wc
        group_params = regrouped.shape[1] * walk
        total_params = group_params * grp
        root_walkers = jnp.sqrt(jnp.float32(WALKERS))
        column_mean = jnp.mean(regrouped, axis=0, keepdims=True)
        centred = (regrouped - column_mean) / root_walkers
        local_gram = jnp.dot(centred, centred.T, precision=lax.Precision.HIGHEST)

        nb = WALKERS // BLOCK
        packed = pack_upper(local_gram, nb)
        n_blocks = packed.shape[0]
        flat = packed.reshape(n_blocks * BLOCK, BLOCK)
        chunk = reduce_scatter(flat, levels)
        per_dev = chunk.shape[0]
        energy_row = jnp.zeros((1, BLOCK), jnp.float32)
        energy_row = energy_row.at[0, : energies.shape[0]].set(energies)
        chunk = jnp.concatenate([chunk, energy_row], axis=0)
        gathered = all_gather(chunk, levels[::-1])
        gathered = gathered.reshape(grp, wc, wx, wz, per_dev + 1, BLOCK)
        whole_packed = gathered[..., :per_dev, :].reshape(n_blocks, BLOCK, BLOCK)
        per_walk = energies.shape[0]
        all_energy = gathered[0, :, :, :, per_dev, :per_walk]
        all_energy = jnp.transpose(all_energy, (1, 2, 0, 3)).reshape(WALKERS)

        whole_gram = unpack_upper(whole_packed, nb)
        scaled_energy = (all_energy - jnp.mean(all_energy)) / root_walkers
        identity_mat = jnp.eye(WALKERS, dtype=jnp.float32)
        lam = damping * total_params
        system = whole_gram + lam * identity_mat
        guess, ok = certified_cg(system, scaled_energy, lam, CG_STEPS, CG_TOL)
        solved = lax.cond(
            ok,
            lambda a, b, g: g,
            lambda a, b, g: cholesky_solve(a, b, nb),
            system,
            scaled_energy,
            guess,
        )
        update = jnp.dot(solved, centred, precision=lax.Precision.HIGHEST)
        return -(total_params / root_walkers) * update

    return on_device


def solution(mesh):
    grp = mesh.shape["grp"]
    walk = mesh.shape["walk"]
    wx, wz, wc = split_walk(walk)
    devices = np.asarray(mesh.devices).reshape(grp, wx, wz, wc)
    fine = Mesh(devices, ("grp",) + WALK_PARTS)
    return jax.shard_map(
        make_on_device((grp, wx, wz, wc)),
        mesh=fine,
        in_specs=(P(WALK_PARTS, "grp"), P(WALK_PARTS)),
        out_specs=P(("grp",) + WALK_PARTS),
        check_vma=False,
    )
```

```python
import jax
import jax.numpy as jnp
import numpy as np
from jax import lax
from jax.sharding import Mesh
from jax.sharding import PartitionSpec as P

WALKERS = 1024
BLOCK = 128
CG_STEPS = 10
CG_TOL = 2e-5


damping = 0.0004

WALK_PARTS = ("wx", "wz", "wc")


def split_walk(walk):
    if walk % 32 == 0 and walk // 32 <= 4:
        return (walk // 32, 16, 2)
    return (1, 1, walk)


def factor_solve(factor, rhs):
    column = rhs[:, None]
    first = lax.linalg.triangular_solve(factor, column, left_side=True, lower=True)
    second = lax.linalg.triangular_solve(
        factor, first, left_side=True, lower=True, transpose_a=True
    )
    return second[:, 0]


def reduce_scatter(x, levels):
    for axis, size in levels:
        rows = x.shape[0]
        parts = x.reshape(size, rows // size, x.shape[1])
        x = lax.all_to_all(parts, axis, 0, 0, tiled=True).sum(0)
    return x


def all_gather(x, levels):
    for axis, size in levels:
        copies = jnp.broadcast_to(x[None], (size,) + x.shape)
        x = lax.all_to_all(copies, axis, 0, 0, tiled=True)
    return x


def upper_pairs(nb):
    return [(i, j) for i in range(nb) for j in range(i, nb)]


def pack_upper(gram, nb):
    blocks = gram.reshape(nb, BLOCK, nb, BLOCK)
    return jnp.stack([blocks[i, :, j, :] for i, j in upper_pairs(nb)])


def unpack_upper(packed, nb):
    where = {pair: k for k, pair in enumerate(upper_pairs(nb))}
    index = np.array(
        [[where[(min(i, j), max(i, j))] for j in range(nb)] for i in range(nb)]
    )
    blocks = packed[index.reshape(-1)].reshape(nb, nb, BLOCK, BLOCK)
    below = np.arange(nb)[:, None] > np.arange(nb)[None, :]
    inner = np.arange(BLOCK)[:, None] > np.arange(BLOCK)[None, :]
    diag = np.eye(nb, dtype=bool)
    mirror = below[:, :, None, None] | (diag[:, :, None, None] & inner[None, None])
    blocks = jnp.where(mirror, jnp.swapaxes(blocks, 2, 3), blocks)
    return jnp.transpose(blocks, (0, 2, 1, 3)).reshape(nb * BLOCK, nb * BLOCK)


def cholesky_solve(system, rhs, nb):
    hi = lax.Precision.HIGHEST
    eye = jnp.eye(BLOCK, dtype=jnp.float32)
    inverses, panels, partial = [], [], []
    for k in range(nb):
        lo, up = k * BLOCK, (k + 1) * BLOCK
        factor = lax.linalg.cholesky(system[lo:up, lo:up], symmetrize_input=False)
        inverse = lax.linalg.triangular_solve(factor, eye, left_side=True, lower=True)
        part = jnp.dot(inverse, rhs[lo:up], precision=hi)
        inverses.append(inverse)
        partial.append(part)
        if k + 1 < nb:
            panel = jnp.dot(system[up:, lo:up], inverse.T, precision=hi)
            panels.append(panel)
            trailing = system[up:, up:] - jnp.dot(panel, panel.T, precision=hi)
            system = system.at[up:, up:].set(trailing)
            rhs = rhs.at[up:].add(-jnp.dot(panel, part, precision=hi))
    solved = [None] * nb
    tail = None
    for k in reversed(range(nb)):
        value = partial[k]
        if tail is not None:
            value = value - jnp.dot(tail, panels[k], precision=hi)
        solved[k] = jnp.dot(value, inverses[k], precision=hi)
        tail = solved[k] if tail is None else jnp.concatenate([solved[k], tail])
    return jnp.concatenate(solved)


def sym_matvec(system, v):
    return jnp.sum(system * v[:, None], axis=0)


def certified_cg(system, rhs, lam, steps, tol):
    hi = lax.Precision.HIGHEST
    eye = np.eye(system.shape[0], dtype=bool)
    inv_diag = 1.0 / jnp.sum(jnp.where(eye, system, 0.0), axis=0)
    x = jnp.zeros_like(rhs)
    r = rhs
    z = r * inv_diag
    p = z
    rz = jnp.dot(r, z, precision=hi)
    for _ in range(steps):
        ap = sym_matvec(system, p)
        alpha = rz / jnp.dot(p, ap, precision=hi)
        x = x + alpha * p
        r = r - alpha * ap
        z = r * inv_diag
        rz_next = jnp.dot(r, z, precision=hi)
        p = z + (rz_next / rz) * p
        rz = rz_next
    ax = sym_matvec(system, x)
    resid = rhs - ax
    energy = jnp.dot(x, ax, precision=hi) - lam * jnp.dot(x, x, precision=hi)
    bound = jnp.dot(resid, resid, precision=hi)
    ok = bound <= (tol * tol) * lam * energy
    return x, ok


def make_on_device(sizes):
    grp, wx, wz, wc = sizes
    levels = [("wc", wc), ("grp", grp), ("wx", wx), ("wz", wz)]
    levels = [(a, n) for a, n in levels if n > 1]
    n_dev = grp * wx * wz * wc

    def on_device(log_grads, energies):
        walk_axes = WALK_PARTS
        regrouped = lax.all_to_all(
            log_grads, walk_axes, split_axis=1, concat_axis=0, tiled=True
        )
        walk = wx * wz * wc
        group_params = regrouped.shape[1] * walk
        total_params = group_params * grp
        root_walkers = jnp.sqrt(jnp.float32(WALKERS))
        column_mean = jnp.mean(regrouped, axis=0, keepdims=True)
        centred = (regrouped - column_mean) / root_walkers
        local_gram = jnp.dot(centred, centred.T, precision=lax.Precision.HIGHEST)

        nb = WALKERS // BLOCK
        packed = pack_upper(local_gram, nb)
        n_blocks = packed.shape[0]
        flat = packed.reshape(n_blocks * BLOCK, BLOCK)
        chunk = reduce_scatter(flat, levels)
        per_dev = chunk.shape[0]
        energy_row = jnp.zeros((1, BLOCK), jnp.float32)
        energy_row = energy_row.at[0, : energies.shape[0]].set(energies)
        chunk = jnp.concatenate([chunk, energy_row], axis=0)
        gathered = all_gather(chunk, levels[::-1])
        names = [a for a, n in levels]
        gathered = gathered.reshape([n for a, n in levels] + [per_dev + 1, BLOCK])
        whole_packed = gathered[..., :per_dev, :].reshape(n_blocks, BLOCK, BLOCK)
        per_walk = energies.shape[0]
        energy = gathered[..., per_dev, :per_walk]
        if "grp" in names:
            energy = jnp.take(energy, 0, axis=names.index("grp"))
            names.remove("grp")
        order = [names.index(a) for a in WALK_PARTS if a in names]
        all_energy = jnp.transpose(energy, order + [len(names)]).reshape(WALKERS)

        whole_gram = unpack_upper(whole_packed, nb)
        scaled_energy = (all_energy - jnp.mean(all_energy)) / root_walkers
        identity_mat = jnp.eye(WALKERS, dtype=jnp.float32)
        lam = damping * total_params
        system = whole_gram + lam * identity_mat
        guess, ok = certified_cg(system, scaled_energy, lam, CG_STEPS, CG_TOL)
        solved = lax.cond(
            ok,
            lambda a, b, g: g,
            lambda a, b, g: cholesky_solve(a, b, nb),
            system,
            scaled_energy,
            guess,
        )
        update = jnp.dot(solved, centred, precision=lax.Precision.HIGHEST)
        return -(total_params / root_walkers) * update

    return on_device


def solution(mesh):
    grp = mesh.shape["grp"]
    walk = mesh.shape["walk"]
    wx, wz, wc = split_walk(walk)
    devices = np.asarray(mesh.devices).reshape(grp, wx, wz, wc)
    fine = Mesh(devices, ("grp",) + WALK_PARTS)
    return jax.shard_map(
        make_on_device((grp, wx, wz, wc)),
        mesh=fine,
        in_specs=(P(WALK_PARTS, "grp"), P(WALK_PARTS)),
        out_specs=P(("grp",) + WALK_PARTS),
        check_vma=False,
    )
```

```python
import jax
import jax.numpy as jnp
import numpy as np
from jax import lax
from jax.sharding import Mesh
from jax.sharding import PartitionSpec as P

WALKERS = 1024
BLOCK = 128
CG_STEPS = 10
CG_TOL = 2e-5


damping = 0.0004

WALK_PARTS = ("wx", "wz", "wc")


def split_walk(walk):
    if walk % 32 == 0 and walk // 32 <= 4:
        return (walk // 32, 16, 2)
    return (1, 1, walk)


def factor_solve(factor, rhs):
    column = rhs[:, None]
    first = lax.linalg.triangular_solve(factor, column, left_side=True, lower=True)
    second = lax.linalg.triangular_solve(
        factor, first, left_side=True, lower=True, transpose_a=True
    )
    return second[:, 0]


def reduce_scatter(x, levels):
    for axis, size in levels:
        rows = x.shape[0]
        parts = x.reshape(size, rows // size, x.shape[1])
        x = lax.all_to_all(parts, axis, 0, 0, tiled=True).sum(0)
    return x


def all_gather(x, levels):
    for axis, size in levels:
        copies = jnp.broadcast_to(x[None], (size,) + x.shape)
        x = lax.all_to_all(copies, axis, 0, 0, tiled=True)
    return x


def regroup(log_grads, sizes):
    wx, wz, wc = sizes
    rows, cols = log_grads.shape
    width = cols // (wx * wz * wc)
    y = log_grads.reshape(rows, wx, wz, wc, width)
    y = jnp.transpose(y, (3, 0, 1, 2, 4))
    y = lax.all_to_all(y, "wc", 0, 0, tiled=True)
    y = jnp.transpose(y, (3, 0, 1, 2, 4))
    y = lax.all_to_all(y, "wz", 0, 0, tiled=True)
    y = jnp.transpose(y, (3, 0, 1, 2, 4))
    y = lax.all_to_all(y, "wx", 0, 0, tiled=True)
    return y.reshape(wx * wz * wc * rows, width)


def upper_pairs(nb):
    return [(i, j) for i in range(nb) for j in range(i, nb)]


def pack_upper(gram, nb):
    blocks = gram.reshape(nb, BLOCK, nb, BLOCK)
    return jnp.stack([blocks[i, :, j, :] for i, j in upper_pairs(nb)])


def unpack_upper(packed, nb):
    where = {pair: k for k, pair in enumerate(upper_pairs(nb))}
    index = np.array(
        [[where[(min(i, j), max(i, j))] for j in range(nb)] for i in range(nb)]
    )
    blocks = packed[index.reshape(-1)].reshape(nb, nb, BLOCK, BLOCK)
    below = np.arange(nb)[:, None] > np.arange(nb)[None, :]
    inner = np.arange(BLOCK)[:, None] > np.arange(BLOCK)[None, :]
    diag = np.eye(nb, dtype=bool)
    mirror = below[:, :, None, None] | (diag[:, :, None, None] & inner[None, None])
    blocks = jnp.where(mirror, jnp.swapaxes(blocks, 2, 3), blocks)
    return jnp.transpose(blocks, (0, 2, 1, 3)).reshape(nb * BLOCK, nb * BLOCK)


def cholesky_solve(system, rhs, nb):
    hi = lax.Precision.HIGHEST
    eye = jnp.eye(BLOCK, dtype=jnp.float32)
    inverses, panels, partial = [], [], []
    for k in range(nb):
        lo, up = k * BLOCK, (k + 1) * BLOCK
        factor = lax.linalg.cholesky(system[lo:up, lo:up], symmetrize_input=False)
        inverse = lax.linalg.triangular_solve(factor, eye, left_side=True, lower=True)
        part = jnp.dot(inverse, rhs[lo:up], precision=hi)
        inverses.append(inverse)
        partial.append(part)
        if k + 1 < nb:
            panel = jnp.dot(system[up:, lo:up], inverse.T, precision=hi)
            panels.append(panel)
            trailing = system[up:, up:] - jnp.dot(panel, panel.T, precision=hi)
            system = system.at[up:, up:].set(trailing)
            rhs = rhs.at[up:].add(-jnp.dot(panel, part, precision=hi))
    solved = [None] * nb
    tail = None
    for k in reversed(range(nb)):
        value = partial[k]
        if tail is not None:
            value = value - jnp.dot(tail, panels[k], precision=hi)
        solved[k] = jnp.dot(value, inverses[k], precision=hi)
        tail = solved[k] if tail is None else jnp.concatenate([solved[k], tail])
    return jnp.concatenate(solved)


def sym_matvec(system, v):
    return jnp.sum(system * v[:, None], axis=0)


def certified_cg(system, rhs, lam, steps, tol):
    hi = lax.Precision.HIGHEST
    eye = np.eye(system.shape[0], dtype=bool)
    inv_diag = 1.0 / jnp.sum(jnp.where(eye, system, 0.0), axis=0)
    x = jnp.zeros_like(rhs)
    r = rhs
    z = r * inv_diag
    p = z
    rz = jnp.dot(r, z, precision=hi)
    for _ in range(steps):
        ap = sym_matvec(system, p)
        alpha = rz / jnp.dot(p, ap, precision=hi)
        x = x + alpha * p
        r = r - alpha * ap
        z = r * inv_diag
        rz_next = jnp.dot(r, z, precision=hi)
        p = z + (rz_next / rz) * p
        rz = rz_next
    ax = sym_matvec(system, x)
    resid = rhs - ax
    energy = jnp.dot(x, ax, precision=hi) - lam * jnp.dot(x, x, precision=hi)
    bound = jnp.dot(resid, resid, precision=hi)
    ok = bound <= (tol * tol) * lam * energy
    return x, ok


def make_on_device(sizes):
    grp, wx, wz, wc = sizes
    levels = [("wc", wc), ("grp", grp), ("wx", wx), ("wz", wz)]
    levels = [(a, n) for a, n in levels if n > 1]
    n_dev = grp * wx * wz * wc

    def on_device(log_grads, energies):
        regrouped = regroup(log_grads, (wx, wz, wc))
        walk = wx * wz * wc
        group_params = regrouped.shape[1] * walk
        total_params = group_params * grp
        root_walkers = jnp.sqrt(jnp.float32(WALKERS))
        column_mean = jnp.mean(regrouped, axis=0, keepdims=True)
        centred = (regrouped - column_mean) / root_walkers
        local_gram = jnp.dot(centred, centred.T, precision=lax.Precision.HIGHEST)

        nb = WALKERS // BLOCK
        packed = pack_upper(local_gram, nb)
        n_blocks = packed.shape[0]
        flat = packed.reshape(n_blocks * BLOCK, BLOCK)
        chunk = reduce_scatter(flat, levels)
        per_dev = chunk.shape[0]
        energy_row = jnp.zeros((1, BLOCK), jnp.float32)
        energy_row = energy_row.at[0, : energies.shape[0]].set(energies)
        chunk = jnp.concatenate([chunk, energy_row], axis=0)
        gathered = all_gather(chunk, levels[::-1])
        names = [a for a, n in levels]
        gathered = gathered.reshape([n for a, n in levels] + [per_dev + 1, BLOCK])
        whole_packed = gathered[..., :per_dev, :].reshape(n_blocks, BLOCK, BLOCK)
        per_walk = energies.shape[0]
        energy = gathered[..., per_dev, :per_walk]
        if "grp" in names:
            energy = jnp.take(energy, 0, axis=names.index("grp"))
            names.remove("grp")
        order = [names.index(a) for a in WALK_PARTS if a in names]
        all_energy = jnp.transpose(energy, order + [len(names)]).reshape(WALKERS)

        whole_gram = unpack_upper(whole_packed, nb)
        scaled_energy = (all_energy - jnp.mean(all_energy)) / root_walkers
        identity_mat = jnp.eye(WALKERS, dtype=jnp.float32)
        lam = damping * total_params
        system = whole_gram + lam * identity_mat
        guess, ok = certified_cg(system, scaled_energy, lam, CG_STEPS, CG_TOL)
        solved = lax.cond(
            ok,
            lambda a, b, g: g,
            lambda a, b, g: cholesky_solve(a, b, nb),
            system,
            scaled_energy,
            guess,
        )
        update = jnp.dot(solved, centred, precision=lax.Precision.HIGHEST)
        return -(total_params / root_walkers) * update

    return on_device


def solution(mesh):
    grp = mesh.shape["grp"]
    walk = mesh.shape["walk"]
    wx, wz, wc = split_walk(walk)
    devices = np.asarray(mesh.devices).reshape(grp, wx, wz, wc)
    fine = Mesh(devices, ("grp",) + WALK_PARTS)
    return jax.shard_map(
        make_on_device((grp, wx, wz, wc)),
        mesh=fine,
        in_specs=(P(WALK_PARTS, "grp"), P(WALK_PARTS)),
        out_specs=P(("grp",) + WALK_PARTS),
        check_vma=False,
    )
```

```python
import jax
import jax.numpy as jnp
import numpy as np
from jax import lax
from jax.experimental import pallas as pl
from jax.experimental.pallas import tpu as pltpu
from jax.sharding import Mesh
from jax.sharding import PartitionSpec as P

WALKERS = 1024
BLOCK = 128
CG_STEPS = 10
CG_TOL = 2e-5


damping = 0.0004

WALK_PARTS = ("wx", "wz", "wc")


def split_walk(walk):
    if walk % 32 == 0 and walk // 32 <= 4:
        return (walk // 32, 16, 2)
    return (1, 1, walk)


def factor_solve(factor, rhs):
    column = rhs[:, None]
    first = lax.linalg.triangular_solve(factor, column, left_side=True, lower=True)
    second = lax.linalg.triangular_solve(
        factor, first, left_side=True, lower=True, transpose_a=True
    )
    return second[:, 0]


def reduce_scatter(x, levels):
    for axis, size in levels:
        rows = x.shape[0]
        parts = x.reshape(size, rows // size, x.shape[1])
        x = lax.all_to_all(parts, axis, 0, 0, tiled=True).sum(0)
    return x


def all_gather(x, levels):
    for axis, size in levels:
        copies = jnp.broadcast_to(x[None], (size,) + x.shape)
        x = lax.all_to_all(copies, axis, 0, 0, tiled=True)
    return x


def upper_pairs(nb):
    return [(i, j) for i in range(nb) for j in range(i, nb)]


def pack_upper(gram, nb):
    blocks = gram.reshape(nb, BLOCK, nb, BLOCK)
    return jnp.stack([blocks[i, :, j, :] for i, j in upper_pairs(nb)])


def unpack_upper(packed, nb):
    where = {pair: k for k, pair in enumerate(upper_pairs(nb))}
    index = np.array(
        [[where[(min(i, j), max(i, j))] for j in range(nb)] for i in range(nb)]
    )
    blocks = packed[index.reshape(-1)].reshape(nb, nb, BLOCK, BLOCK)
    below = np.arange(nb)[:, None] > np.arange(nb)[None, :]
    inner = np.arange(BLOCK)[:, None] > np.arange(BLOCK)[None, :]
    diag = np.eye(nb, dtype=bool)
    mirror = below[:, :, None, None] | (diag[:, :, None, None] & inner[None, None])
    blocks = jnp.where(mirror, jnp.swapaxes(blocks, 2, 3), blocks)
    return jnp.transpose(blocks, (0, 2, 1, 3)).reshape(nb * BLOCK, nb * BLOCK)


def cholesky_solve(system, rhs, nb):
    hi = lax.Precision.HIGHEST
    eye = jnp.eye(BLOCK, dtype=jnp.float32)
    inverses, panels, partial = [], [], []
    for k in range(nb):
        lo, up = k * BLOCK, (k + 1) * BLOCK
        factor = lax.linalg.cholesky(system[lo:up, lo:up], symmetrize_input=False)
        inverse = lax.linalg.triangular_solve(factor, eye, left_side=True, lower=True)
        part = jnp.dot(inverse, rhs[lo:up], precision=hi)
        inverses.append(inverse)
        partial.append(part)
        if k + 1 < nb:
            panel = jnp.dot(system[up:, lo:up], inverse.T, precision=hi)
            panels.append(panel)
            trailing = system[up:, up:] - jnp.dot(panel, panel.T, precision=hi)
            system = system.at[up:, up:].set(trailing)
            rhs = rhs.at[up:].add(-jnp.dot(panel, part, precision=hi))
    solved = [None] * nb
    tail = None
    for k in reversed(range(nb)):
        value = partial[k]
        if tail is not None:
            value = value - jnp.dot(tail, panels[k], precision=hi)
        solved[k] = jnp.dot(value, inverses[k], precision=hi)
        tail = solved[k] if tail is None else jnp.concatenate([solved[k], tail])
    return jnp.concatenate(solved)


def sym_matvec(system, v):
    return jnp.sum(system * v[:, None], axis=0)


def certified_cg(system, rhs, lam, steps, tol):
    hi = lax.Precision.HIGHEST
    eye = np.eye(system.shape[0], dtype=bool)
    inv_diag = 1.0 / jnp.sum(jnp.where(eye, system, 0.0), axis=0)
    x = jnp.zeros_like(rhs)
    r = rhs
    z = r * inv_diag
    p = z
    rz = jnp.dot(r, z, precision=hi)
    for _ in range(steps):
        ap = sym_matvec(system, p)
        alpha = rz / jnp.dot(p, ap, precision=hi)
        x = x + alpha * p
        r = r - alpha * ap
        z = r * inv_diag
        rz_next = jnp.dot(r, z, precision=hi)
        p = z + (rz_next / rz) * p
        rz = rz_next
    ax = sym_matvec(system, x)
    resid = rhs - ax
    energy = jnp.dot(x, ax, precision=hi) - lam * jnp.dot(x, x, precision=hi)
    bound = jnp.dot(resid, resid, precision=hi)
    ok = bound <= (tol * tol) * lam * energy
    return x, ok


INTERPRET = False


def cg_kernel(lam, steps, a_ref, b_ref, d_ref, x_ref, st_ref, pc_ref):
    n = a_ref.shape[0]
    chunk = BLOCK

    def matvec(p_row):
        pc_ref[...] = jnp.transpose(jnp.broadcast_to(p_row, (8, n)))
        acc = jnp.zeros((1, n), jnp.float32)
        for c in range(n // chunk):
            blk = a_ref[c * chunk : (c + 1) * chunk, :]
            col = pc_ref[c * chunk : (c + 1) * chunk, 0:1]
            acc = acc + jnp.sum(blk * col, axis=0, keepdims=True)
        return acc

    b_row = b_ref[...]
    d_row = d_ref[...]
    z_row = b_row * d_row
    rz = jnp.sum(b_row * z_row, axis=1, keepdims=True)

    def body(_, carry):
        x_row, r_row, p_row, rz = carry
        ap_row = matvec(p_row)
        alpha = rz / jnp.sum(p_row * ap_row, axis=1, keepdims=True)
        x_row = x_row + alpha * p_row
        r_row = r_row - alpha * ap_row
        z_row = r_row * d_row
        rz_next = jnp.sum(r_row * z_row, axis=1, keepdims=True)
        p_row = z_row + (rz_next / rz) * p_row
        return x_row, r_row, p_row, rz_next

    x0 = jnp.zeros((1, n), jnp.float32)
    x_row = lax.fori_loop(0, steps, body, (x0, b_row, z_row, rz))[0]
    ax_row = matvec(x_row)
    resid = b_row - ax_row
    bound = jnp.sum(resid * resid, axis=1, keepdims=True)
    energy = jnp.sum(x_row * ax_row, axis=1, keepdims=True) - lam * jnp.sum(
        x_row * x_row, axis=1, keepdims=True
    )
    x_ref[...] = x_row
    lane = lax.broadcasted_iota(jnp.int32, (1, 128), 1)
    st_ref[...] = jnp.where(lane == 0, bound, jnp.where(lane == 1, energy, 0.0))


def kernel_cg(system, rhs, lam, steps, tol):
    n = system.shape[0]
    eye = np.eye(n, dtype=bool)
    inv_diag = 1.0 / jnp.sum(jnp.where(eye, system, 0.0), axis=0)
    body = lambda *refs: cg_kernel(lam, steps, *refs)
    x, st = pl.pallas_call(
        body,
        out_shape=(
            jax.ShapeDtypeStruct((1, n), jnp.float32),
            jax.ShapeDtypeStruct((1, 128), jnp.float32),
        ),
        scratch_shapes=[pltpu.VMEM((n, 8), jnp.float32)],
        interpret=INTERPRET,
    )(system, rhs[None, :], inv_diag[None, :])
    ok = st[0, 0] <= (tol * tol) * lam * st[0, 1]
    return x[0], ok


def make_on_device(sizes):
    grp, wx, wz, wc = sizes
    levels = [("wc", wc), ("grp", grp), ("wx", wx), ("wz", wz)]
    levels = [(a, n) for a, n in levels if n > 1]
    n_dev = grp * wx * wz * wc

    def on_device(log_grads, energies):
        walk_axes = WALK_PARTS
        regrouped = lax.all_to_all(
            log_grads, walk_axes, split_axis=1, concat_axis=0, tiled=True
        )
        walk = wx * wz * wc
        group_params = regrouped.shape[1] * walk
        total_params = group_params * grp
        root_walkers = jnp.sqrt(jnp.float32(WALKERS))
        column_mean = jnp.mean(regrouped, axis=0, keepdims=True)
        centred = (regrouped - column_mean) / root_walkers
        local_gram = jnp.dot(centred, centred.T, precision=lax.Precision.HIGHEST)

        nb = WALKERS // BLOCK
        packed = pack_upper(local_gram, nb)
        n_blocks = packed.shape[0]
        flat = packed.reshape(n_blocks * BLOCK, BLOCK)
        chunk = reduce_scatter(flat, levels)
        per_dev = chunk.shape[0]
        energy_row = jnp.zeros((1, BLOCK), jnp.float32)
        energy_row = energy_row.at[0, : energies.shape[0]].set(energies)
        chunk = jnp.concatenate([chunk, energy_row], axis=0)
        gathered = all_gather(chunk, levels[::-1])
        names = [a for a, n in levels]
        gathered = gathered.reshape([n for a, n in levels] + [per_dev + 1, BLOCK])
        whole_packed = gathered[..., :per_dev, :].reshape(n_blocks, BLOCK, BLOCK)
        per_walk = energies.shape[0]
        energy = gathered[..., per_dev, :per_walk]
        if "grp" in names:
            energy = jnp.take(energy, 0, axis=names.index("grp"))
            names.remove("grp")
        order = [names.index(a) for a in WALK_PARTS if a in names]
        all_energy = jnp.transpose(energy, order + [len(names)]).reshape(WALKERS)

        whole_gram = unpack_upper(whole_packed, nb)
        scaled_energy = (all_energy - jnp.mean(all_energy)) / root_walkers
        identity_mat = jnp.eye(WALKERS, dtype=jnp.float32)
        lam = damping * total_params
        system = whole_gram + lam * identity_mat
        guess, ok = kernel_cg(system, scaled_energy, lam, CG_STEPS, CG_TOL)
        solved = lax.cond(
            ok,
            lambda a, b, g: g,
            lambda a, b, g: cholesky_solve(a, b, nb),
            system,
            scaled_energy,
            guess,
        )
        update = jnp.dot(solved, centred, precision=lax.Precision.HIGHEST)
        return -(total_params / root_walkers) * update

    return on_device


def solution(mesh):
    grp = mesh.shape["grp"]
    walk = mesh.shape["walk"]
    wx, wz, wc = split_walk(walk)
    devices = np.asarray(mesh.devices).reshape(grp, wx, wz, wc)
    fine = Mesh(devices, ("grp",) + WALK_PARTS)
    return jax.shard_map(
        make_on_device((grp, wx, wz, wc)),
        mesh=fine,
        in_specs=(P(WALK_PARTS, "grp"), P(WALK_PARTS)),
        out_specs=P(("grp",) + WALK_PARTS),
        check_vma=False,
    )
```

```python
import jax
import jax.numpy as jnp
import numpy as np
from jax import lax
from jax.experimental import pallas as pl
from jax.experimental.pallas import tpu as pltpu
from jax.sharding import Mesh
from jax.sharding import PartitionSpec as P

WALKERS = 1024
BLOCK = 128
CG_STEPS = 10
CG_TOL = 2e-5


damping = 0.0004

WALK_PARTS = ("wx", "wz", "wc")


def split_walk(walk):
    if walk % 32 == 0 and walk // 32 <= 4:
        return (walk // 32, 16, 2)
    return (1, 1, walk)


def factor_solve(factor, rhs):
    column = rhs[:, None]
    first = lax.linalg.triangular_solve(factor, column, left_side=True, lower=True)
    second = lax.linalg.triangular_solve(
        factor, first, left_side=True, lower=True, transpose_a=True
    )
    return second[:, 0]


def reduce_scatter(x, levels):
    for axis, size in levels:
        rows = x.shape[0]
        parts = x.reshape(size, rows // size, x.shape[1])
        x = lax.all_to_all(parts, axis, 0, 0, tiled=True).sum(0)
    return x


def all_gather(x, levels):
    for axis, size in levels:
        copies = jnp.broadcast_to(x[None], (size,) + x.shape)
        x = lax.all_to_all(copies, axis, 0, 0, tiled=True)
    return x


def upper_pairs(nb):
    return [(i, j) for i in range(nb) for j in range(i, nb)]


def pack_upper(gram, nb):
    blocks = gram.reshape(nb, BLOCK, nb, BLOCK)
    return jnp.stack([blocks[i, :, j, :] for i, j in upper_pairs(nb)])


def unpack_upper(packed, nb):
    where = {pair: k for k, pair in enumerate(upper_pairs(nb))}
    index = np.array(
        [[where[(min(i, j), max(i, j))] for j in range(nb)] for i in range(nb)]
    )
    blocks = packed[index.reshape(-1)].reshape(nb, nb, BLOCK, BLOCK)
    below = np.arange(nb)[:, None] > np.arange(nb)[None, :]
    inner = np.arange(BLOCK)[:, None] > np.arange(BLOCK)[None, :]
    diag = np.eye(nb, dtype=bool)
    mirror = below[:, :, None, None] | (diag[:, :, None, None] & inner[None, None])
    blocks = jnp.where(mirror, jnp.swapaxes(blocks, 2, 3), blocks)
    return jnp.transpose(blocks, (0, 2, 1, 3)).reshape(nb * BLOCK, nb * BLOCK)


def cholesky_solve(system, rhs, nb):
    hi = lax.Precision.HIGHEST
    eye = jnp.eye(BLOCK, dtype=jnp.float32)
    inverses, panels, partial = [], [], []
    for k in range(nb):
        lo, up = k * BLOCK, (k + 1) * BLOCK
        factor = lax.linalg.cholesky(system[lo:up, lo:up], symmetrize_input=False)
        inverse = lax.linalg.triangular_solve(factor, eye, left_side=True, lower=True)
        part = jnp.dot(inverse, rhs[lo:up], precision=hi)
        inverses.append(inverse)
        partial.append(part)
        if k + 1 < nb:
            panel = jnp.dot(system[up:, lo:up], inverse.T, precision=hi)
            panels.append(panel)
            trailing = system[up:, up:] - jnp.dot(panel, panel.T, precision=hi)
            system = system.at[up:, up:].set(trailing)
            rhs = rhs.at[up:].add(-jnp.dot(panel, part, precision=hi))
    solved = [None] * nb
    tail = None
    for k in reversed(range(nb)):
        value = partial[k]
        if tail is not None:
            value = value - jnp.dot(tail, panels[k], precision=hi)
        solved[k] = jnp.dot(value, inverses[k], precision=hi)
        tail = solved[k] if tail is None else jnp.concatenate([solved[k], tail])
    return jnp.concatenate(solved)


def sym_matvec(system, v):
    return jnp.sum(system * v[:, None], axis=0)


def certified_cg(system, rhs, lam, steps, tol):
    hi = lax.Precision.HIGHEST
    eye = np.eye(system.shape[0], dtype=bool)
    inv_diag = 1.0 / jnp.sum(jnp.where(eye, system, 0.0), axis=0)
    x = jnp.zeros_like(rhs)
    r = rhs
    z = r * inv_diag
    p = z
    rz = jnp.dot(r, z, precision=hi)
    for _ in range(steps):
        ap = sym_matvec(system, p)
        alpha = rz / jnp.dot(p, ap, precision=hi)
        x = x + alpha * p
        r = r - alpha * ap
        z = r * inv_diag
        rz_next = jnp.dot(r, z, precision=hi)
        p = z + (rz_next / rz) * p
        rz = rz_next
    ax = sym_matvec(system, x)
    resid = rhs - ax
    energy = jnp.dot(x, ax, precision=hi) - lam * jnp.dot(x, x, precision=hi)
    bound = jnp.dot(resid, resid, precision=hi)
    ok = bound <= (tol * tol) * lam * energy
    return x, ok


INTERPRET = False


def cg_kernel(lam, steps, nb, u_ref, b_ref, d_ref, x_ref, st_ref, pc_ref):
    n = nb * BLOCK
    pairs = upper_pairs(nb)

    def matvec(p_row):
        pc_ref[...] = jnp.transpose(jnp.broadcast_to(p_row, (8, n)))
        rows = [jnp.zeros((1, BLOCK), jnp.float32) for _ in range(nb)]
        cols = [jnp.zeros((BLOCK, 1), jnp.float32) for _ in range(nb)]
        for k, (i, j) in enumerate(pairs):
            blk = u_ref[k]
            p_i = pc_ref[i * BLOCK : (i + 1) * BLOCK, 0:1]
            rows[j] = rows[j] + jnp.sum(blk * p_i, axis=0, keepdims=True)
            if i < j:
                p_j = p_row[:, j * BLOCK : (j + 1) * BLOCK]
                cols[i] = cols[i] + jnp.sum(blk * p_j, axis=1, keepdims=True)
        col = jnp.concatenate(cols, axis=0)
        col_row = jnp.transpose(jnp.broadcast_to(col, (n, 8)))[0:1, :]
        return jnp.concatenate(rows, axis=1) + col_row

    b_row = b_ref[...]
    d_row = d_ref[...]
    z_row = b_row * d_row
    rz = jnp.sum(b_row * z_row, axis=1, keepdims=True)

    def body(_, carry):
        x_row, r_row, p_row, rz = carry
        ap_row = matvec(p_row)
        alpha = rz / jnp.sum(p_row * ap_row, axis=1, keepdims=True)
        x_row = x_row + alpha * p_row
        r_row = r_row - alpha * ap_row
        z_row = r_row * d_row
        rz_next = jnp.sum(r_row * z_row, axis=1, keepdims=True)
        p_row = z_row + (rz_next / rz) * p_row
        return x_row, r_row, p_row, rz_next

    x0 = jnp.zeros((1, n), jnp.float32)
    x_row = lax.fori_loop(0, steps, body, (x0, b_row, z_row, rz))[0]
    ax_row = matvec(x_row)
    resid = b_row - ax_row
    bound = jnp.sum(resid * resid, axis=1, keepdims=True)
    energy = jnp.sum(x_row * ax_row, axis=1, keepdims=True) - lam * jnp.sum(
        x_row * x_row, axis=1, keepdims=True
    )
    x_ref[...] = x_row
    lane = lax.broadcasted_iota(jnp.int32, (1, 128), 1)
    st_ref[...] = jnp.where(lane == 0, bound, jnp.where(lane == 1, energy, 0.0))


def damp_packed(packed, nb, lam):
    where = {pair: k for k, pair in enumerate(upper_pairs(nb))}
    on_diag = np.zeros((len(where), 1, 1), np.float32)
    for i in range(nb):
        on_diag[where[(i, i)]] = 1.0
    eye = np.eye(BLOCK, dtype=np.float32)[None]
    return packed + (lam * on_diag) * eye


def kernel_cg(packed, rhs, lam, steps, tol, nb):
    n = nb * BLOCK
    where = {pair: k for k, pair in enumerate(upper_pairs(nb))}
    diag_blocks = packed[np.array([where[(i, i)] for i in range(nb)])]
    eye = np.eye(BLOCK, dtype=bool)[None]
    inv_diag = 1.0 / jnp.sum(jnp.where(eye, diag_blocks, 0.0), axis=1).reshape(n)
    body = lambda *refs: cg_kernel(lam, steps, nb, *refs)
    x, st = pl.pallas_call(
        body,
        out_shape=(
            jax.ShapeDtypeStruct((1, n), jnp.float32),
            jax.ShapeDtypeStruct((1, 128), jnp.float32),
        ),
        scratch_shapes=[pltpu.VMEM((n, 8), jnp.float32)],
        interpret=INTERPRET,
    )(packed, rhs[None, :], inv_diag[None, :])
    ok = st[0, 0] <= (tol * tol) * lam * st[0, 1]
    return x[0], ok


def make_on_device(sizes):
    grp, wx, wz, wc = sizes
    levels = [("wc", wc), ("grp", grp), ("wx", wx), ("wz", wz)]
    levels = [(a, n) for a, n in levels if n > 1]
    n_dev = grp * wx * wz * wc

    def on_device(log_grads, energies):
        walk_axes = WALK_PARTS
        regrouped = lax.all_to_all(
            log_grads, walk_axes, split_axis=1, concat_axis=0, tiled=True
        )
        walk = wx * wz * wc
        group_params = regrouped.shape[1] * walk
        total_params = group_params * grp
        root_walkers = jnp.sqrt(jnp.float32(WALKERS))
        column_mean = jnp.mean(regrouped, axis=0, keepdims=True)
        centred = (regrouped - column_mean) / root_walkers
        local_gram = jnp.dot(centred, centred.T, precision=lax.Precision.HIGHEST)

        nb = WALKERS // BLOCK
        packed = pack_upper(local_gram, nb)
        n_blocks = packed.shape[0]
        flat = packed.reshape(n_blocks * BLOCK, BLOCK)
        chunk = reduce_scatter(flat, levels)
        per_dev = chunk.shape[0]
        energy_row = jnp.zeros((1, BLOCK), jnp.float32)
        energy_row = energy_row.at[0, : energies.shape[0]].set(energies)
        chunk = jnp.concatenate([chunk, energy_row], axis=0)
        gathered = all_gather(chunk, levels[::-1])
        names = [a for a, n in levels]
        gathered = gathered.reshape([n for a, n in levels] + [per_dev + 1, BLOCK])
        whole_packed = gathered[..., :per_dev, :].reshape(n_blocks, BLOCK, BLOCK)
        per_walk = energies.shape[0]
        energy = gathered[..., per_dev, :per_walk]
        if "grp" in names:
            energy = jnp.take(energy, 0, axis=names.index("grp"))
            names.remove("grp")
        order = [names.index(a) for a in WALK_PARTS if a in names]
        all_energy = jnp.transpose(energy, order + [len(names)]).reshape(WALKERS)

        scaled_energy = (all_energy - jnp.mean(all_energy)) / root_walkers
        lam = damping * total_params
        system_packed = damp_packed(whole_packed, nb, lam)
        guess, ok = kernel_cg(system_packed, scaled_energy, lam, CG_STEPS, CG_TOL, nb)
        solved = lax.cond(
            ok,
            lambda a, b, g: g,
            lambda a, b, g: cholesky_solve(unpack_upper(a, nb), b, nb),
            system_packed,
            scaled_energy,
            guess,
        )
        update = jnp.dot(solved, centred, precision=lax.Precision.HIGHEST)
        return -(total_params / root_walkers) * update

    return on_device


def solution(mesh):
    grp = mesh.shape["grp"]
    walk = mesh.shape["walk"]
    wx, wz, wc = split_walk(walk)
    devices = np.asarray(mesh.devices).reshape(grp, wx, wz, wc)
    fine = Mesh(devices, ("grp",) + WALK_PARTS)
    return jax.shard_map(
        make_on_device((grp, wx, wz, wc)),
        mesh=fine,
        in_specs=(P(WALK_PARTS, "grp"), P(WALK_PARTS)),
        out_specs=P(("grp",) + WALK_PARTS),
        check_vma=False,
    )
```

```python
import jax
import jax.numpy as jnp
import numpy as np
from jax import lax
from jax.experimental import pallas as pl
from jax.experimental.pallas import tpu as pltpu
from jax.sharding import Mesh
from jax.sharding import PartitionSpec as P

WALKERS = 1024
BLOCK = 128
CG_STEPS = 10
CG_TOL = 2e-5


damping = 0.0004

WALK_PARTS = ("wx", "wz", "wc")


def split_walk(walk):
    if walk % 32 == 0 and walk // 32 <= 4:
        return (walk // 32, 16, 2)
    return (1, 1, walk)


def factor_solve(factor, rhs):
    column = rhs[:, None]
    first = lax.linalg.triangular_solve(factor, column, left_side=True, lower=True)
    second = lax.linalg.triangular_solve(
        factor, first, left_side=True, lower=True, transpose_a=True
    )
    return second[:, 0]


def reduce_scatter(x, levels):
    for axis, size in levels:
        rows = x.shape[0]
        parts = x.reshape(size, rows // size, x.shape[1])
        x = lax.all_to_all(parts, axis, 0, 0, tiled=True).sum(0)
    return x


def all_gather(x, levels):
    for axis, size in levels:
        copies = jnp.broadcast_to(x[None], (size,) + x.shape)
        x = lax.all_to_all(copies, axis, 0, 0, tiled=True)
    return x


def upper_pairs(nb):
    return [(i, j) for i in range(nb) for j in range(i, nb)]


def pack_upper(gram, nb):
    blocks = gram.reshape(nb, BLOCK, nb, BLOCK)
    return jnp.stack([blocks[i, :, j, :] for i, j in upper_pairs(nb)])


def unpack_upper(packed, nb):
    where = {pair: k for k, pair in enumerate(upper_pairs(nb))}
    index = np.array(
        [[where[(min(i, j), max(i, j))] for j in range(nb)] for i in range(nb)]
    )
    blocks = packed[index.reshape(-1)].reshape(nb, nb, BLOCK, BLOCK)
    below = np.arange(nb)[:, None] > np.arange(nb)[None, :]
    inner = np.arange(BLOCK)[:, None] > np.arange(BLOCK)[None, :]
    diag = np.eye(nb, dtype=bool)
    mirror = below[:, :, None, None] | (diag[:, :, None, None] & inner[None, None])
    blocks = jnp.where(mirror, jnp.swapaxes(blocks, 2, 3), blocks)
    return jnp.transpose(blocks, (0, 2, 1, 3)).reshape(nb * BLOCK, nb * BLOCK)


def cholesky_solve(system, rhs, nb):
    hi = lax.Precision.HIGHEST
    eye = jnp.eye(BLOCK, dtype=jnp.float32)
    inverses, panels, partial = [], [], []
    for k in range(nb):
        lo, up = k * BLOCK, (k + 1) * BLOCK
        factor = lax.linalg.cholesky(system[lo:up, lo:up], symmetrize_input=False)
        inverse = lax.linalg.triangular_solve(factor, eye, left_side=True, lower=True)
        part = jnp.dot(inverse, rhs[lo:up], precision=hi)
        inverses.append(inverse)
        partial.append(part)
        if k + 1 < nb:
            panel = jnp.dot(system[up:, lo:up], inverse.T, precision=hi)
            panels.append(panel)
            trailing = system[up:, up:] - jnp.dot(panel, panel.T, precision=hi)
            system = system.at[up:, up:].set(trailing)
            rhs = rhs.at[up:].add(-jnp.dot(panel, part, precision=hi))
    solved = [None] * nb
    tail = None
    for k in reversed(range(nb)):
        value = partial[k]
        if tail is not None:
            value = value - jnp.dot(tail, panels[k], precision=hi)
        solved[k] = jnp.dot(value, inverses[k], precision=hi)
        tail = solved[k] if tail is None else jnp.concatenate([solved[k], tail])
    return jnp.concatenate(solved)


def sym_matvec(system, v):
    return jnp.sum(system * v[:, None], axis=0)


def certified_cg(system, rhs, lam, steps, tol):
    hi = lax.Precision.HIGHEST
    eye = np.eye(system.shape[0], dtype=bool)
    inv_diag = 1.0 / jnp.sum(jnp.where(eye, system, 0.0), axis=0)
    x = jnp.zeros_like(rhs)
    r = rhs
    z = r * inv_diag
    p = z
    rz = jnp.dot(r, z, precision=hi)
    for _ in range(steps):
        ap = sym_matvec(system, p)
        alpha = rz / jnp.dot(p, ap, precision=hi)
        x = x + alpha * p
        r = r - alpha * ap
        z = r * inv_diag
        rz_next = jnp.dot(r, z, precision=hi)
        p = z + (rz_next / rz) * p
        rz = rz_next
    ax = sym_matvec(system, x)
    resid = rhs - ax
    energy = jnp.dot(x, ax, precision=hi) - lam * jnp.dot(x, x, precision=hi)
    bound = jnp.dot(resid, resid, precision=hi)
    ok = bound <= (tol * tol) * lam * energy
    return x, ok


INTERPRET = False


def cg_kernel(lam, steps, nb, u_ref, b_ref, d_ref, x_ref, st_ref, pc_ref, lt_ref):
    n = nb * BLOCK
    pairs = upper_pairs(nb)
    for k, (i, j) in enumerate(pairs):
        if i < j:
            lt_ref[k] = jnp.transpose(u_ref[k])

    def matvec(p_row):
        pc_ref[...] = jnp.transpose(jnp.broadcast_to(p_row, (8, n)))
        rows = [jnp.zeros((1, BLOCK), jnp.float32) for _ in range(nb)]
        for k, (i, j) in enumerate(pairs):
            p_i = pc_ref[i * BLOCK : (i + 1) * BLOCK, 0:1]
            rows[j] = rows[j] + jnp.sum(u_ref[k] * p_i, axis=0, keepdims=True)
            if i < j:
                p_j = pc_ref[j * BLOCK : (j + 1) * BLOCK, 0:1]
                rows[i] = rows[i] + jnp.sum(lt_ref[k] * p_j, axis=0, keepdims=True)
        return jnp.concatenate(rows, axis=1)

    b_row = b_ref[...]
    d_row = d_ref[...]
    z_row = b_row * d_row
    rz = jnp.sum(b_row * z_row, axis=1, keepdims=True)

    def body(_, carry):
        x_row, r_row, p_row, rz = carry
        ap_row = matvec(p_row)
        alpha = rz / jnp.sum(p_row * ap_row, axis=1, keepdims=True)
        x_row = x_row + alpha * p_row
        r_row = r_row - alpha * ap_row
        z_row = r_row * d_row
        rz_next = jnp.sum(r_row * z_row, axis=1, keepdims=True)
        p_row = z_row + (rz_next / rz) * p_row
        return x_row, r_row, p_row, rz_next

    x0 = jnp.zeros((1, n), jnp.float32)
    x_row = lax.fori_loop(0, steps, body, (x0, b_row, z_row, rz))[0]
    ax_row = matvec(x_row)
    resid = b_row - ax_row
    bound = jnp.sum(resid * resid, axis=1, keepdims=True)
    energy = jnp.sum(x_row * ax_row, axis=1, keepdims=True) - lam * jnp.sum(
        x_row * x_row, axis=1, keepdims=True
    )
    x_ref[...] = x_row
    lane = lax.broadcasted_iota(jnp.int32, (1, 128), 1)
    st_ref[...] = jnp.where(lane == 0, bound, jnp.where(lane == 1, energy, 0.0))


def damp_packed(packed, nb, lam):
    where = {pair: k for k, pair in enumerate(upper_pairs(nb))}
    on_diag = np.zeros((len(where), 1, 1), np.float32)
    for i in range(nb):
        on_diag[where[(i, i)]] = 1.0
    eye = np.eye(BLOCK, dtype=np.float32)[None]
    return packed + (lam * on_diag) * eye


def kernel_cg(packed, rhs, lam, steps, tol, nb):
    n = nb * BLOCK
    where = {pair: k for k, pair in enumerate(upper_pairs(nb))}
    diag_blocks = packed[np.array([where[(i, i)] for i in range(nb)])]
    eye = np.eye(BLOCK, dtype=bool)[None]
    inv_diag = 1.0 / jnp.sum(jnp.where(eye, diag_blocks, 0.0), axis=1).reshape(n)
    body = lambda *refs: cg_kernel(lam, steps, nb, *refs)
    x, st = pl.pallas_call(
        body,
        out_shape=(
            jax.ShapeDtypeStruct((1, n), jnp.float32),
            jax.ShapeDtypeStruct((1, 128), jnp.float32),
        ),
        scratch_shapes=[
            pltpu.VMEM((n, 8), jnp.float32),
            pltpu.VMEM(packed.shape, jnp.float32),
        ],
        interpret=INTERPRET,
    )(packed, rhs[None, :], inv_diag[None, :])
    ok = st[0, 0] <= (tol * tol) * lam * st[0, 1]
    return x[0], ok


def make_on_device(sizes):
    grp, wx, wz, wc = sizes
    levels = [("wc", wc), ("grp", grp), ("wx", wx), ("wz", wz)]
    levels = [(a, n) for a, n in levels if n > 1]
    n_dev = grp * wx * wz * wc

    def on_device(log_grads, energies):
        walk_axes = WALK_PARTS
        regrouped = lax.all_to_all(
            log_grads, walk_axes, split_axis=1, concat_axis=0, tiled=True
        )
        walk = wx * wz * wc
        group_params = regrouped.shape[1] * walk
        total_params = group_params * grp
        root_walkers = jnp.sqrt(jnp.float32(WALKERS))
        column_mean = jnp.mean(regrouped, axis=0, keepdims=True)
        centred = (regrouped - column_mean) / root_walkers
        local_gram = jnp.dot(centred, centred.T, precision=lax.Precision.HIGHEST)

        nb = WALKERS // BLOCK
        packed = pack_upper(local_gram, nb)
        n_blocks = packed.shape[0]
        flat = packed.reshape(n_blocks * BLOCK, BLOCK)
        chunk = reduce_scatter(flat, levels)
        per_dev = chunk.shape[0]
        energy_row = jnp.zeros((1, BLOCK), jnp.float32)
        energy_row = energy_row.at[0, : energies.shape[0]].set(energies)
        chunk = jnp.concatenate([chunk, energy_row], axis=0)
        gathered = all_gather(chunk, levels[::-1])
        names = [a for a, n in levels]
        gathered = gathered.reshape([n for a, n in levels] + [per_dev + 1, BLOCK])
        whole_packed = gathered[..., :per_dev, :].reshape(n_blocks, BLOCK, BLOCK)
        per_walk = energies.shape[0]
        energy = gathered[..., per_dev, :per_walk]
        if "grp" in names:
            energy = jnp.take(energy, 0, axis=names.index("grp"))
            names.remove("grp")
        order = [names.index(a) for a in WALK_PARTS if a in names]
        all_energy = jnp.transpose(energy, order + [len(names)]).reshape(WALKERS)

        scaled_energy = (all_energy - jnp.mean(all_energy)) / root_walkers
        lam = damping * total_params
        system_packed = damp_packed(whole_packed, nb, lam)
        guess, ok = kernel_cg(system_packed, scaled_energy, lam, CG_STEPS, CG_TOL, nb)
        solved = lax.cond(
            ok,
            lambda a, b, g: g,
            lambda a, b, g: cholesky_solve(unpack_upper(a, nb), b, nb),
            system_packed,
            scaled_energy,
            guess,
        )
        update = jnp.dot(solved, centred, precision=lax.Precision.HIGHEST)
        return -(total_params / root_walkers) * update

    return on_device


def solution(mesh):
    grp = mesh.shape["grp"]
    walk = mesh.shape["walk"]
    wx, wz, wc = split_walk(walk)
    devices = np.asarray(mesh.devices).reshape(grp, wx, wz, wc)
    fine = Mesh(devices, ("grp",) + WALK_PARTS)
    return jax.shard_map(
        make_on_device((grp, wx, wz, wc)),
        mesh=fine,
        in_specs=(P(WALK_PARTS, "grp"), P(WALK_PARTS)),
        out_specs=P(("grp",) + WALK_PARTS),
        check_vma=False,
    )
```

```python
import jax
import jax.numpy as jnp
import numpy as np
from jax import lax
from jax.experimental import pallas as pl
from jax.experimental.pallas import tpu as pltpu
from jax.sharding import Mesh
from jax.sharding import PartitionSpec as P

WALKERS = 1024
BLOCK = 128
CG_STEPS = 10
CG_TOL = 2e-5


damping = 0.0004

WALK_PARTS = ("wx", "wz", "wc")


def split_walk(walk):
    if walk % 32 == 0 and walk // 32 <= 4:
        return (walk // 32, 16, 2)
    return (1, 1, walk)


def factor_solve(factor, rhs):
    column = rhs[:, None]
    first = lax.linalg.triangular_solve(factor, column, left_side=True, lower=True)
    second = lax.linalg.triangular_solve(
        factor, first, left_side=True, lower=True, transpose_a=True
    )
    return second[:, 0]


def reduce_scatter(x, levels):
    for axis, size in levels:
        rows = x.shape[0]
        parts = x.reshape(size, rows // size, x.shape[1])
        x = lax.all_to_all(parts, axis, 0, 0, tiled=True).sum(0)
    return x


def all_gather(x, levels):
    for axis, size in levels:
        copies = jnp.broadcast_to(x[None], (size,) + x.shape)
        x = lax.all_to_all(copies, axis, 0, 0, tiled=True)
    return x


def upper_pairs(nb):
    return [(i, j) for i in range(nb) for j in range(i, nb)]


def pack_upper(gram, nb):
    blocks = gram.reshape(nb, BLOCK, nb, BLOCK)
    return jnp.stack([blocks[i, :, j, :] for i, j in upper_pairs(nb)])


def unpack_upper(packed, nb):
    where = {pair: k for k, pair in enumerate(upper_pairs(nb))}
    index = np.array(
        [[where[(min(i, j), max(i, j))] for j in range(nb)] for i in range(nb)]
    )
    blocks = packed[index.reshape(-1)].reshape(nb, nb, BLOCK, BLOCK)
    below = np.arange(nb)[:, None] > np.arange(nb)[None, :]
    inner = np.arange(BLOCK)[:, None] > np.arange(BLOCK)[None, :]
    diag = np.eye(nb, dtype=bool)
    mirror = below[:, :, None, None] | (diag[:, :, None, None] & inner[None, None])
    blocks = jnp.where(mirror, jnp.swapaxes(blocks, 2, 3), blocks)
    return jnp.transpose(blocks, (0, 2, 1, 3)).reshape(nb * BLOCK, nb * BLOCK)


def cholesky_solve(system, rhs, nb):
    hi = lax.Precision.HIGHEST
    eye = jnp.eye(BLOCK, dtype=jnp.float32)
    inverses, panels, partial = [], [], []
    for k in range(nb):
        lo, up = k * BLOCK, (k + 1) * BLOCK
        factor = lax.linalg.cholesky(system[lo:up, lo:up], symmetrize_input=False)
        inverse = lax.linalg.triangular_solve(factor, eye, left_side=True, lower=True)
        part = jnp.dot(inverse, rhs[lo:up], precision=hi)
        inverses.append(inverse)
        partial.append(part)
        if k + 1 < nb:
            panel = jnp.dot(system[up:, lo:up], inverse.T, precision=hi)
            panels.append(panel)
            trailing = system[up:, up:] - jnp.dot(panel, panel.T, precision=hi)
            system = system.at[up:, up:].set(trailing)
            rhs = rhs.at[up:].add(-jnp.dot(panel, part, precision=hi))
    solved = [None] * nb
    tail = None
    for k in reversed(range(nb)):
        value = partial[k]
        if tail is not None:
            value = value - jnp.dot(tail, panels[k], precision=hi)
        solved[k] = jnp.dot(value, inverses[k], precision=hi)
        tail = solved[k] if tail is None else jnp.concatenate([solved[k], tail])
    return jnp.concatenate(solved)


def sym_matvec(system, v):
    return jnp.sum(system * v[:, None], axis=0)


def certified_cg(system, rhs, lam, steps, tol):
    hi = lax.Precision.HIGHEST
    eye = np.eye(system.shape[0], dtype=bool)
    inv_diag = 1.0 / jnp.sum(jnp.where(eye, system, 0.0), axis=0)
    x = jnp.zeros_like(rhs)
    r = rhs
    z = r * inv_diag
    p = z
    rz = jnp.dot(r, z, precision=hi)
    for _ in range(steps):
        ap = sym_matvec(system, p)
        alpha = rz / jnp.dot(p, ap, precision=hi)
        x = x + alpha * p
        r = r - alpha * ap
        z = r * inv_diag
        rz_next = jnp.dot(r, z, precision=hi)
        p = z + (rz_next / rz) * p
        rz = rz_next
    ax = sym_matvec(system, x)
    resid = rhs - ax
    energy = jnp.dot(x, ax, precision=hi) - lam * jnp.dot(x, x, precision=hi)
    bound = jnp.dot(resid, resid, precision=hi)
    ok = bound <= (tol * tol) * lam * energy
    return x, ok


INTERPRET = False


def cg_kernel(lam, steps, nb, u_ref, b_ref, x_ref, st_ref, pc_ref, lt_ref):
    n = nb * BLOCK
    pairs = upper_pairs(nb)
    for k, (i, j) in enumerate(pairs):
        if i < j:
            lt_ref[k] = jnp.transpose(u_ref[k])

    def matvec(p_row):
        pc_ref[...] = jnp.transpose(jnp.broadcast_to(p_row, (8, n)))
        rows = [jnp.zeros((1, BLOCK), jnp.float32) for _ in range(nb)]
        for k, (i, j) in enumerate(pairs):
            p_i = pc_ref[i * BLOCK : (i + 1) * BLOCK, 0:1]
            rows[j] = rows[j] + jnp.sum(u_ref[k] * p_i, axis=0, keepdims=True)
            if i < j:
                p_j = pc_ref[j * BLOCK : (j + 1) * BLOCK, 0:1]
                rows[i] = rows[i] + jnp.sum(lt_ref[k] * p_j, axis=0, keepdims=True)
        return jnp.concatenate(rows, axis=1)

    b_row = b_ref[...]
    where = {pair: k for k, pair in enumerate(pairs)}
    eye = lax.broadcasted_iota(jnp.int32, (BLOCK, BLOCK), 0) == lax.broadcasted_iota(
        jnp.int32, (BLOCK, BLOCK), 1
    )
    diag = [
        jnp.sum(jnp.where(eye, u_ref[where[(i, i)]], 0.0), axis=0, keepdims=True)
        for i in range(nb)
    ]
    d_row = 1.0 / jnp.concatenate(diag, axis=1)
    z_row = b_row * d_row
    rz = jnp.sum(b_row * z_row, axis=1, keepdims=True)

    def body(_, carry):
        x_row, r_row, p_row, rz = carry
        ap_row = matvec(p_row)
        alpha = rz / jnp.sum(p_row * ap_row, axis=1, keepdims=True)
        x_row = x_row + alpha * p_row
        r_row = r_row - alpha * ap_row
        z_row = r_row * d_row
        rz_next = jnp.sum(r_row * z_row, axis=1, keepdims=True)
        p_row = z_row + (rz_next / rz) * p_row
        return x_row, r_row, p_row, rz_next

    x0 = jnp.zeros((1, n), jnp.float32)
    x_row = lax.fori_loop(0, steps, body, (x0, b_row, z_row, rz))[0]
    ax_row = matvec(x_row)
    resid = b_row - ax_row
    bound = jnp.sum(resid * resid, axis=1, keepdims=True)
    energy = jnp.sum(x_row * ax_row, axis=1, keepdims=True) - lam * jnp.sum(
        x_row * x_row, axis=1, keepdims=True
    )
    x_ref[...] = x_row
    lane = lax.broadcasted_iota(jnp.int32, (1, 128), 1)
    st_ref[...] = jnp.where(lane == 0, bound, jnp.where(lane == 1, energy, 0.0))


def damp_packed(packed, nb, lam):
    where = {pair: k for k, pair in enumerate(upper_pairs(nb))}
    on_diag = np.zeros((len(where), 1, 1), np.float32)
    for i in range(nb):
        on_diag[where[(i, i)]] = 1.0
    eye = np.eye(BLOCK, dtype=np.float32)[None]
    return packed + (lam * on_diag) * eye


def kernel_cg(packed, rhs, lam, steps, tol, nb):
    n = nb * BLOCK
    body = lambda *refs: cg_kernel(lam, steps, nb, *refs)
    x, st = pl.pallas_call(
        body,
        out_shape=(
            jax.ShapeDtypeStruct((1, n), jnp.float32),
            jax.ShapeDtypeStruct((1, 128), jnp.float32),
        ),
        scratch_shapes=[
            pltpu.VMEM((n, 8), jnp.float32),
            pltpu.VMEM(packed.shape, jnp.float32),
        ],
        interpret=INTERPRET,
    )(packed, rhs[None, :])
    ok = st[0, 0] <= (tol * tol) * lam * st[0, 1]
    return x[0], ok


def make_on_device(sizes):
    grp, wx, wz, wc = sizes
    levels = [("wc", wc), ("grp", grp), ("wx", wx), ("wz", wz)]
    levels = [(a, n) for a, n in levels if n > 1]
    n_dev = grp * wx * wz * wc

    def on_device(log_grads, energies):
        walk_axes = WALK_PARTS
        regrouped = lax.all_to_all(
            log_grads, walk_axes, split_axis=1, concat_axis=0, tiled=True
        )
        walk = wx * wz * wc
        group_params = regrouped.shape[1] * walk
        total_params = group_params * grp
        root_walkers = jnp.sqrt(jnp.float32(WALKERS))
        column_mean = jnp.mean(regrouped, axis=0, keepdims=True)
        centred = (regrouped - column_mean) / root_walkers
        local_gram = jnp.dot(centred, centred.T, precision=lax.Precision.HIGHEST)

        nb = WALKERS // BLOCK
        packed = pack_upper(local_gram, nb)
        n_blocks = packed.shape[0]
        flat = packed.reshape(n_blocks * BLOCK, BLOCK)
        chunk = reduce_scatter(flat, levels)
        per_dev = chunk.shape[0]
        energy_row = jnp.zeros((1, BLOCK), jnp.float32)
        energy_row = energy_row.at[0, : energies.shape[0]].set(energies)
        chunk = jnp.concatenate([chunk, energy_row], axis=0)
        gathered = all_gather(chunk, levels[::-1])
        names = [a for a, n in levels]
        gathered = gathered.reshape([n for a, n in levels] + [per_dev + 1, BLOCK])
        whole_packed = gathered[..., :per_dev, :].reshape(n_blocks, BLOCK, BLOCK)
        per_walk = energies.shape[0]
        energy = gathered[..., per_dev, :per_walk]
        if "grp" in names:
            energy = jnp.take(energy, 0, axis=names.index("grp"))
            names.remove("grp")
        order = [names.index(a) for a in WALK_PARTS if a in names]
        all_energy = jnp.transpose(energy, order + [len(names)]).reshape(WALKERS)

        scaled_energy = (all_energy - jnp.mean(all_energy)) / root_walkers
        lam = damping * total_params
        system_packed = damp_packed(whole_packed, nb, lam)
        guess, ok = kernel_cg(system_packed, scaled_energy, lam, CG_STEPS, CG_TOL, nb)
        solved = lax.cond(
            ok,
            lambda a, b, g: g,
            lambda a, b, g: cholesky_solve(unpack_upper(a, nb), b, nb),
            system_packed,
            scaled_energy,
            guess,
        )
        update = jnp.dot(solved, centred, precision=lax.Precision.HIGHEST)
        return -(total_params / root_walkers) * update

    return on_device


def solution(mesh):
    grp = mesh.shape["grp"]
    walk = mesh.shape["walk"]
    wx, wz, wc = split_walk(walk)
    devices = np.asarray(mesh.devices).reshape(grp, wx, wz, wc)
    fine = Mesh(devices, ("grp",) + WALK_PARTS)
    return jax.shard_map(
        make_on_device((grp, wx, wz, wc)),
        mesh=fine,
        in_specs=(P(WALK_PARTS, "grp"), P(WALK_PARTS)),
        out_specs=P(("grp",) + WALK_PARTS),
        check_vma=False,
    )
```

```python
import jax
import jax.numpy as jnp
import numpy as np
from jax import lax
from jax.experimental import pallas as pl
from jax.experimental.pallas import tpu as pltpu
from jax.sharding import Mesh
from jax.sharding import PartitionSpec as P

WALKERS = 1024
BLOCK = 128
CG_STEPS = 10
CG_TOL = 2e-5


damping = 0.0004

WALK_PARTS = ("wx", "wz", "wc")


def split_walk(walk):
    if walk % 32 == 0 and walk // 32 <= 4:
        return (walk // 32, 16, 2)
    return (1, 1, walk)


def factor_solve(factor, rhs):
    column = rhs[:, None]
    first = lax.linalg.triangular_solve(factor, column, left_side=True, lower=True)
    second = lax.linalg.triangular_solve(
        factor, first, left_side=True, lower=True, transpose_a=True
    )
    return second[:, 0]


def reduce_scatter(x, levels):
    for axis, size in levels:
        rows = x.shape[0]
        parts = x.reshape(size, rows // size, x.shape[1])
        x = lax.all_to_all(parts, axis, 0, 0, tiled=True).sum(0)
    return x


def all_gather(x, levels):
    for axis, size in levels:
        copies = jnp.broadcast_to(x[None], (size,) + x.shape)
        x = lax.all_to_all(copies, axis, 0, 0, tiled=True)
    return x


def upper_pairs(nb):
    return [(i, j) for i in range(nb) for j in range(i, nb)]


def pack_upper(gram, nb):
    blocks = gram.reshape(nb, BLOCK, nb, BLOCK)
    return jnp.stack([blocks[i, :, j, :] for i, j in upper_pairs(nb)])


def unpack_upper(packed, nb):
    where = {pair: k for k, pair in enumerate(upper_pairs(nb))}
    index = np.array(
        [[where[(min(i, j), max(i, j))] for j in range(nb)] for i in range(nb)]
    )
    blocks = packed[index.reshape(-1)].reshape(nb, nb, BLOCK, BLOCK)
    below = np.arange(nb)[:, None] > np.arange(nb)[None, :]
    inner = np.arange(BLOCK)[:, None] > np.arange(BLOCK)[None, :]
    diag = np.eye(nb, dtype=bool)
    mirror = below[:, :, None, None] | (diag[:, :, None, None] & inner[None, None])
    blocks = jnp.where(mirror, jnp.swapaxes(blocks, 2, 3), blocks)
    return jnp.transpose(blocks, (0, 2, 1, 3)).reshape(nb * BLOCK, nb * BLOCK)


def cholesky_solve(system, rhs, nb):
    hi = lax.Precision.HIGHEST
    eye = jnp.eye(BLOCK, dtype=jnp.float32)
    inverses, panels, partial = [], [], []
    for k in range(nb):
        lo, up = k * BLOCK, (k + 1) * BLOCK
        factor = lax.linalg.cholesky(system[lo:up, lo:up], symmetrize_input=False)
        inverse = lax.linalg.triangular_solve(factor, eye, left_side=True, lower=True)
        part = jnp.dot(inverse, rhs[lo:up], precision=hi)
        inverses.append(inverse)
        partial.append(part)
        if k + 1 < nb:
            panel = jnp.dot(system[up:, lo:up], inverse.T, precision=hi)
            panels.append(panel)
            trailing = system[up:, up:] - jnp.dot(panel, panel.T, precision=hi)
            system = system.at[up:, up:].set(trailing)
            rhs = rhs.at[up:].add(-jnp.dot(panel, part, precision=hi))
    solved = [None] * nb
    tail = None
    for k in reversed(range(nb)):
        value = partial[k]
        if tail is not None:
            value = value - jnp.dot(tail, panels[k], precision=hi)
        solved[k] = jnp.dot(value, inverses[k], precision=hi)
        tail = solved[k] if tail is None else jnp.concatenate([solved[k], tail])
    return jnp.concatenate(solved)


def sym_matvec(system, v):
    return jnp.sum(system * v[:, None], axis=0)


def certified_cg(system, rhs, lam, steps, tol):
    hi = lax.Precision.HIGHEST
    eye = np.eye(system.shape[0], dtype=bool)
    inv_diag = 1.0 / jnp.sum(jnp.where(eye, system, 0.0), axis=0)
    x = jnp.zeros_like(rhs)
    r = rhs
    z = r * inv_diag
    p = z
    rz = jnp.dot(r, z, precision=hi)
    for _ in range(steps):
        ap = sym_matvec(system, p)
        alpha = rz / jnp.dot(p, ap, precision=hi)
        x = x + alpha * p
        r = r - alpha * ap
        z = r * inv_diag
        rz_next = jnp.dot(r, z, precision=hi)
        p = z + (rz_next / rz) * p
        rz = rz_next
    ax = sym_matvec(system, x)
    resid = rhs - ax
    energy = jnp.dot(x, ax, precision=hi) - lam * jnp.dot(x, x, precision=hi)
    bound = jnp.dot(resid, resid, precision=hi)
    ok = bound <= (tol * tol) * lam * energy
    return x, ok


INTERPRET = False


def cg_kernel(lam, steps, nb, u_ref, b_ref, x_ref, st_ref, pc_ref, lt_ref):
    n = nb * BLOCK
    pairs = upper_pairs(nb)
    for k, (i, j) in enumerate(pairs):
        if i < j:
            lt_ref[k] = jnp.transpose(u_ref[k])

    def matvec(p_row):
        pc_ref[...] = jnp.transpose(jnp.broadcast_to(p_row, (8, n)))
        rows = [jnp.zeros((1, BLOCK), jnp.float32) for _ in range(nb)]
        for k, (i, j) in enumerate(pairs):
            p_i = pc_ref[i * BLOCK : (i + 1) * BLOCK, 0:1]
            rows[j] = rows[j] + jnp.sum(u_ref[k] * p_i, axis=0, keepdims=True)
            if i < j:
                p_j = pc_ref[j * BLOCK : (j + 1) * BLOCK, 0:1]
                rows[i] = rows[i] + jnp.sum(lt_ref[k] * p_j, axis=0, keepdims=True)
        return jnp.concatenate(rows, axis=1) + lam * p_row

    b_row = b_ref[...]
    where = {pair: k for k, pair in enumerate(pairs)}
    eye = lax.broadcasted_iota(jnp.int32, (BLOCK, BLOCK), 0) == lax.broadcasted_iota(
        jnp.int32, (BLOCK, BLOCK), 1
    )
    diag = [
        jnp.sum(jnp.where(eye, u_ref[where[(i, i)]], 0.0), axis=0, keepdims=True)
        for i in range(nb)
    ]
    d_row = 1.0 / (jnp.concatenate(diag, axis=1) + lam)
    z_row = b_row * d_row
    rz = jnp.sum(b_row * z_row, axis=1, keepdims=True)

    def body(_, carry):
        x_row, r_row, p_row, rz = carry
        ap_row = matvec(p_row)
        alpha = rz / jnp.sum(p_row * ap_row, axis=1, keepdims=True)
        x_row = x_row + alpha * p_row
        r_row = r_row - alpha * ap_row
        z_row = r_row * d_row
        rz_next = jnp.sum(r_row * z_row, axis=1, keepdims=True)
        p_row = z_row + (rz_next / rz) * p_row
        return x_row, r_row, p_row, rz_next

    x0 = jnp.zeros((1, n), jnp.float32)
    x_row = lax.fori_loop(0, steps, body, (x0, b_row, z_row, rz))[0]
    ax_row = matvec(x_row)
    resid = b_row - ax_row
    bound = jnp.sum(resid * resid, axis=1, keepdims=True)
    energy = jnp.sum(x_row * ax_row, axis=1, keepdims=True) - lam * jnp.sum(
        x_row * x_row, axis=1, keepdims=True
    )
    x_ref[...] = x_row
    lane = lax.broadcasted_iota(jnp.int32, (1, 128), 1)
    st_ref[...] = jnp.where(lane == 0, bound, jnp.where(lane == 1, energy, 0.0))


def damp_packed(packed, nb, lam):
    where = {pair: k for k, pair in enumerate(upper_pairs(nb))}
    on_diag = np.zeros((len(where), 1, 1), np.float32)
    for i in range(nb):
        on_diag[where[(i, i)]] = 1.0
    eye = np.eye(BLOCK, dtype=np.float32)[None]
    return packed + (lam * on_diag) * eye


def kernel_cg(packed, rhs, lam, steps, tol, nb):
    n = nb * BLOCK
    body = lambda *refs: cg_kernel(lam, steps, nb, *refs)
    x, st = pl.pallas_call(
        body,
        out_shape=(
            jax.ShapeDtypeStruct((1, n), jnp.float32),
            jax.ShapeDtypeStruct((1, 128), jnp.float32),
        ),
        scratch_shapes=[
            pltpu.VMEM((n, 8), jnp.float32),
            pltpu.VMEM(packed.shape, jnp.float32),
        ],
        interpret=INTERPRET,
    )(packed, rhs[None, :])
    ok = st[0, 0] <= (tol * tol) * lam * st[0, 1]
    return x[0], ok


def make_on_device(sizes):
    grp, wx, wz, wc = sizes
    levels = [("wc", wc), ("grp", grp), ("wx", wx), ("wz", wz)]
    levels = [(a, n) for a, n in levels if n > 1]
    n_dev = grp * wx * wz * wc

    def on_device(log_grads, energies):
        walk_axes = WALK_PARTS
        regrouped = lax.all_to_all(
            log_grads, walk_axes, split_axis=1, concat_axis=0, tiled=True
        )
        walk = wx * wz * wc
        group_params = regrouped.shape[1] * walk
        total_params = group_params * grp
        root_walkers = jnp.sqrt(jnp.float32(WALKERS))
        column_mean = jnp.mean(regrouped, axis=0, keepdims=True)
        centred = (regrouped - column_mean) / root_walkers
        local_gram = jnp.dot(centred, centred.T, precision=lax.Precision.HIGHEST)

        nb = WALKERS // BLOCK
        packed = pack_upper(local_gram, nb)
        n_blocks = packed.shape[0]
        flat = packed.reshape(n_blocks * BLOCK, BLOCK)
        chunk = reduce_scatter(flat, levels)
        per_dev = chunk.shape[0]
        energy_row = jnp.zeros((1, BLOCK), jnp.float32)
        energy_row = energy_row.at[0, : energies.shape[0]].set(energies)
        chunk = jnp.concatenate([chunk, energy_row], axis=0)
        gathered = all_gather(chunk, levels[::-1])
        names = [a for a, n in levels]
        gathered = gathered.reshape([n for a, n in levels] + [per_dev + 1, BLOCK])
        whole_packed = gathered[..., :per_dev, :].reshape(n_blocks, BLOCK, BLOCK)
        per_walk = energies.shape[0]
        energy = gathered[..., per_dev, :per_walk]
        if "grp" in names:
            energy = jnp.take(energy, 0, axis=names.index("grp"))
            names.remove("grp")
        order = [names.index(a) for a in WALK_PARTS if a in names]
        all_energy = jnp.transpose(energy, order + [len(names)]).reshape(WALKERS)

        scaled_energy = (all_energy - jnp.mean(all_energy)) / root_walkers
        lam = damping * total_params
        guess, ok = kernel_cg(whole_packed, scaled_energy, lam, CG_STEPS, CG_TOL, nb)
        solved = lax.cond(
            ok,
            lambda a, b, g: g,
            lambda a, b, g: cholesky_solve(
                unpack_upper(damp_packed(a, nb, lam), nb), b, nb
            ),
            whole_packed,
            scaled_energy,
            guess,
        )
        update = jnp.dot(solved, centred, precision=lax.Precision.HIGHEST)
        return -(total_params / root_walkers) * update

    return on_device


def solution(mesh):
    grp = mesh.shape["grp"]
    walk = mesh.shape["walk"]
    wx, wz, wc = split_walk(walk)
    devices = np.asarray(mesh.devices).reshape(grp, wx, wz, wc)
    fine = Mesh(devices, ("grp",) + WALK_PARTS)
    return jax.shard_map(
        make_on_device((grp, wx, wz, wc)),
        mesh=fine,
        in_specs=(P(WALK_PARTS, "grp"), P(WALK_PARTS)),
        out_specs=P(("grp",) + WALK_PARTS),
        check_vma=False,
    )
```

```python
import jax
import jax.numpy as jnp
import numpy as np
from jax import lax
from jax.experimental import pallas as pl
from jax.experimental.pallas import tpu as pltpu
from jax.sharding import Mesh
from jax.sharding import PartitionSpec as P

WALKERS = 1024
BLOCK = 128
CG_STEPS = 10
CG_TOL = 2e-5


damping = 0.0004

WALK_PARTS = ("wx", "wz", "wc")


def split_walk(walk):
    if walk % 32 == 0 and walk // 32 <= 4:
        return (walk // 32, 16, 2)
    return (1, 1, walk)


def factor_solve(factor, rhs):
    column = rhs[:, None]
    first = lax.linalg.triangular_solve(factor, column, left_side=True, lower=True)
    second = lax.linalg.triangular_solve(
        factor, first, left_side=True, lower=True, transpose_a=True
    )
    return second[:, 0]


def reduce_scatter(x, levels):
    for axis, size in levels:
        rows = x.shape[0]
        parts = x.reshape(size, rows // size, x.shape[1])
        x = lax.all_to_all(parts, axis, 0, 0, tiled=True).sum(0)
    return x


def all_gather(x, levels):
    for axis, size in levels:
        copies = jnp.broadcast_to(x[None], (size,) + x.shape)
        x = lax.all_to_all(copies, axis, 0, 0, tiled=True)
    return x


def upper_pairs(nb):
    return [(i, j) for i in range(nb) for j in range(i, nb)]


def pack_upper(gram, nb):
    blocks = gram.reshape(nb, BLOCK, nb, BLOCK)
    return jnp.stack([blocks[i, :, j, :] for i, j in upper_pairs(nb)])


def unpack_upper(packed, nb):
    where = {pair: k for k, pair in enumerate(upper_pairs(nb))}
    index = np.array(
        [[where[(min(i, j), max(i, j))] for j in range(nb)] for i in range(nb)]
    )
    blocks = packed[index.reshape(-1)].reshape(nb, nb, BLOCK, BLOCK)
    below = np.arange(nb)[:, None] > np.arange(nb)[None, :]
    inner = np.arange(BLOCK)[:, None] > np.arange(BLOCK)[None, :]
    diag = np.eye(nb, dtype=bool)
    mirror = below[:, :, None, None] | (diag[:, :, None, None] & inner[None, None])
    blocks = jnp.where(mirror, jnp.swapaxes(blocks, 2, 3), blocks)
    return jnp.transpose(blocks, (0, 2, 1, 3)).reshape(nb * BLOCK, nb * BLOCK)


def cholesky_solve(system, rhs, nb):
    hi = lax.Precision.HIGHEST
    eye = jnp.eye(BLOCK, dtype=jnp.float32)
    inverses, panels, partial = [], [], []
    for k in range(nb):
        lo, up = k * BLOCK, (k + 1) * BLOCK
        factor = lax.linalg.cholesky(system[lo:up, lo:up], symmetrize_input=False)
        inverse = lax.linalg.triangular_solve(factor, eye, left_side=True, lower=True)
        part = jnp.dot(inverse, rhs[lo:up], precision=hi)
        inverses.append(inverse)
        partial.append(part)
        if k + 1 < nb:
            panel = jnp.dot(system[up:, lo:up], inverse.T, precision=hi)
            panels.append(panel)
            trailing = system[up:, up:] - jnp.dot(panel, panel.T, precision=hi)
            system = system.at[up:, up:].set(trailing)
            rhs = rhs.at[up:].add(-jnp.dot(panel, part, precision=hi))
    solved = [None] * nb
    tail = None
    for k in reversed(range(nb)):
        value = partial[k]
        if tail is not None:
            value = value - jnp.dot(tail, panels[k], precision=hi)
        solved[k] = jnp.dot(value, inverses[k], precision=hi)
        tail = solved[k] if tail is None else jnp.concatenate([solved[k], tail])
    return jnp.concatenate(solved)


def sym_matvec(system, v):
    return jnp.sum(system * v[:, None], axis=0)


def certified_cg(system, rhs, lam, steps, tol):
    hi = lax.Precision.HIGHEST
    eye = np.eye(system.shape[0], dtype=bool)
    inv_diag = 1.0 / jnp.sum(jnp.where(eye, system, 0.0), axis=0)
    x = jnp.zeros_like(rhs)
    r = rhs
    z = r * inv_diag
    p = z
    rz = jnp.dot(r, z, precision=hi)
    for _ in range(steps):
        ap = sym_matvec(system, p)
        alpha = rz / jnp.dot(p, ap, precision=hi)
        x = x + alpha * p
        r = r - alpha * ap
        z = r * inv_diag
        rz_next = jnp.dot(r, z, precision=hi)
        p = z + (rz_next / rz) * p
        rz = rz_next
    ax = sym_matvec(system, x)
    resid = rhs - ax
    energy = jnp.dot(x, ax, precision=hi) - lam * jnp.dot(x, x, precision=hi)
    bound = jnp.dot(resid, resid, precision=hi)
    ok = bound <= (tol * tol) * lam * energy
    return x, ok


INTERPRET = False


def cg_kernel(lam, steps, nb, u_ref, b_ref, x_ref, st_ref, pc_ref, lt_ref):
    n = nb * BLOCK
    pairs = upper_pairs(nb)
    for k, (i, j) in enumerate(pairs):
        if i < j:
            lt_ref[k] = jnp.transpose(u_ref[k])

    def matvec(p_row):
        pc_ref[...] = jnp.transpose(jnp.broadcast_to(p_row, (8, n)))
        rows = [jnp.zeros((1, BLOCK), jnp.float32) for _ in range(nb)]
        for k, (i, j) in enumerate(pairs):
            p_i = pc_ref[i * BLOCK : (i + 1) * BLOCK, 0:1]
            rows[j] = rows[j] + jnp.sum(u_ref[k] * p_i, axis=0, keepdims=True)
            if i < j:
                p_j = pc_ref[j * BLOCK : (j + 1) * BLOCK, 0:1]
                rows[i] = rows[i] + jnp.sum(lt_ref[k] * p_j, axis=0, keepdims=True)
        return jnp.concatenate(rows, axis=1) + lam * p_row

    b_row = b_ref[...]
    where = {pair: k for k, pair in enumerate(pairs)}
    eye = lax.broadcasted_iota(jnp.int32, (BLOCK, BLOCK), 0) == lax.broadcasted_iota(
        jnp.int32, (BLOCK, BLOCK), 1
    )
    diag = [
        jnp.sum(jnp.where(eye, u_ref[where[(i, i)]], 0.0), axis=0, keepdims=True)
        for i in range(nb)
    ]
    d_row = 1.0 / (jnp.concatenate(diag, axis=1) + lam)
    z_row = b_row * d_row
    rz = jnp.sum(b_row * z_row, axis=1, keepdims=True)

    def body(_, carry):
        x_row, r_row, p_row, rz = carry
        ap_row = matvec(p_row)
        alpha = rz / jnp.sum(p_row * ap_row, axis=1, keepdims=True)
        x_row = x_row + alpha * p_row
        r_row = r_row - alpha * ap_row
        z_row = r_row * d_row
        rz_next = jnp.sum(r_row * z_row, axis=1, keepdims=True)
        p_row = z_row + (rz_next / rz) * p_row
        return x_row, r_row, p_row, rz_next

    x0 = jnp.zeros((1, n), jnp.float32)
    x_row = lax.fori_loop(0, steps, body, (x0, b_row, z_row, rz))[0]
    ax_row = matvec(x_row)
    resid = b_row - ax_row
    bound = jnp.sum(resid * resid, axis=1, keepdims=True)
    energy = jnp.sum(x_row * ax_row, axis=1, keepdims=True) - lam * jnp.sum(
        x_row * x_row, axis=1, keepdims=True
    )
    x_ref[...] = x_row
    lane = lax.broadcasted_iota(jnp.int32, (1, 128), 1)
    st_ref[...] = jnp.where(lane == 0, bound, jnp.where(lane == 1, energy, 0.0))


def damp_packed(packed, nb, lam):
    where = {pair: k for k, pair in enumerate(upper_pairs(nb))}
    on_diag = np.zeros((len(where), 1, 1), np.float32)
    for i in range(nb):
        on_diag[where[(i, i)]] = 1.0
    eye = np.eye(BLOCK, dtype=np.float32)[None]
    return packed + (lam * on_diag) * eye


def kernel_cg(packed, rhs, lam, steps, tol, nb):
    n = nb * BLOCK
    body = lambda *refs: cg_kernel(lam, steps, nb, *refs)
    x, st = pl.pallas_call(
        body,
        out_shape=(
            jax.ShapeDtypeStruct((1, n), jnp.float32),
            jax.ShapeDtypeStruct((1, 128), jnp.float32),
        ),
        scratch_shapes=[
            pltpu.VMEM((n, 8), jnp.float32),
            pltpu.VMEM(packed.shape, jnp.float32),
        ],
        interpret=INTERPRET,
    )(packed, rhs[None, :])
    ok = st[0, 0] <= (tol * tol) * lam * st[0, 1]
    return x[0], ok


def make_on_device(sizes):
    grp, wx, wz, wc = sizes
    levels = [("wc", wc), ("grp", grp), ("wz", wz), ("wx", wx)]
    levels = [(a, n) for a, n in levels if n > 1]
    n_dev = grp * wx * wz * wc

    def on_device(log_grads, energies):
        walk_axes = WALK_PARTS
        regrouped = lax.all_to_all(
            log_grads, walk_axes, split_axis=1, concat_axis=0, tiled=True
        )
        walk = wx * wz * wc
        group_params = regrouped.shape[1] * walk
        total_params = group_params * grp
        root_walkers = jnp.sqrt(jnp.float32(WALKERS))
        column_mean = jnp.mean(regrouped, axis=0, keepdims=True)
        centred = (regrouped - column_mean) / root_walkers
        local_gram = jnp.dot(centred, centred.T, precision=lax.Precision.HIGHEST)

        nb = WALKERS // BLOCK
        packed = pack_upper(local_gram, nb)
        n_blocks = packed.shape[0]
        flat = packed.reshape(n_blocks * BLOCK, BLOCK)
        chunk = reduce_scatter(flat, levels)
        per_dev = chunk.shape[0]
        energy_row = jnp.zeros((1, BLOCK), jnp.float32)
        energy_row = energy_row.at[0, : energies.shape[0]].set(energies)
        chunk = jnp.concatenate([chunk, energy_row], axis=0)
        gathered = all_gather(chunk, levels[::-1])
        names = [a for a, n in levels]
        gathered = gathered.reshape([n for a, n in levels] + [per_dev + 1, BLOCK])
        whole_packed = gathered[..., :per_dev, :].reshape(n_blocks, BLOCK, BLOCK)
        per_walk = energies.shape[0]
        energy = gathered[..., per_dev, :per_walk]
        if "grp" in names:
            energy = jnp.take(energy, 0, axis=names.index("grp"))
            names.remove("grp")
        order = [names.index(a) for a in WALK_PARTS if a in names]
        all_energy = jnp.transpose(energy, order + [len(names)]).reshape(WALKERS)

        scaled_energy = (all_energy - jnp.mean(all_energy)) / root_walkers
        lam = damping * total_params
        guess, ok = kernel_cg(whole_packed, scaled_energy, lam, CG_STEPS, CG_TOL, nb)
        solved = lax.cond(
            ok,
            lambda a, b, g: g,
            lambda a, b, g: cholesky_solve(
                unpack_upper(damp_packed(a, nb, lam), nb), b, nb
            ),
            whole_packed,
            scaled_energy,
            guess,
        )
        update = jnp.dot(solved, centred, precision=lax.Precision.HIGHEST)
        return -(total_params / root_walkers) * update

    return on_device


def solution(mesh):
    grp = mesh.shape["grp"]
    walk = mesh.shape["walk"]
    wx, wz, wc = split_walk(walk)
    devices = np.asarray(mesh.devices).reshape(grp, wx, wz, wc)
    fine = Mesh(devices, ("grp",) + WALK_PARTS)
    return jax.shard_map(
        make_on_device((grp, wx, wz, wc)),
        mesh=fine,
        in_specs=(P(WALK_PARTS, "grp"), P(WALK_PARTS)),
        out_specs=P(("grp",) + WALK_PARTS),
        check_vma=False,
    )
```

```python
import jax
import jax.numpy as jnp
import numpy as np
from jax import lax
from jax.experimental import pallas as pl
from jax.experimental.pallas import tpu as pltpu
from jax.sharding import Mesh
from jax.sharding import PartitionSpec as P

WALKERS = 1024
BLOCK = 128
CG_STEPS = 10
CG_TOL = 2e-5


damping = 0.0004

WALK_PARTS = ("wx", "wz", "wc")


def split_walk(walk):
    if walk % 32 == 0 and walk // 32 <= 4:
        return (walk // 32, 16, 2)
    return (1, 1, walk)


def factor_solve(factor, rhs):
    column = rhs[:, None]
    first = lax.linalg.triangular_solve(factor, column, left_side=True, lower=True)
    second = lax.linalg.triangular_solve(
        factor, first, left_side=True, lower=True, transpose_a=True
    )
    return second[:, 0]


def reduce_scatter(x, levels):
    for axis, size in levels:
        rows = x.shape[0]
        parts = x.reshape(size, rows // size, x.shape[1])
        x = lax.all_to_all(parts, axis, 0, 0, tiled=True).sum(0)
    return x


def all_gather(x, levels):
    for axis, size in levels:
        copies = jnp.broadcast_to(x[None], (size,) + x.shape)
        x = lax.all_to_all(copies, axis, 0, 0, tiled=True)
    return x


def upper_pairs(nb):
    return [(i, j) for i in range(nb) for j in range(i, nb)]


def pack_upper(gram, nb):
    blocks = gram.reshape(nb, BLOCK, nb, BLOCK)
    return jnp.stack([blocks[i, :, j, :] for i, j in upper_pairs(nb)])


def unpack_upper(packed, nb):
    where = {pair: k for k, pair in enumerate(upper_pairs(nb))}
    index = np.array(
        [[where[(min(i, j), max(i, j))] for j in range(nb)] for i in range(nb)]
    )
    blocks = packed[index.reshape(-1)].reshape(nb, nb, BLOCK, BLOCK)
    below = np.arange(nb)[:, None] > np.arange(nb)[None, :]
    inner = np.arange(BLOCK)[:, None] > np.arange(BLOCK)[None, :]
    diag = np.eye(nb, dtype=bool)
    mirror = below[:, :, None, None] | (diag[:, :, None, None] & inner[None, None])
    blocks = jnp.where(mirror, jnp.swapaxes(blocks, 2, 3), blocks)
    return jnp.transpose(blocks, (0, 2, 1, 3)).reshape(nb * BLOCK, nb * BLOCK)


def cholesky_solve(system, rhs, nb):
    hi = lax.Precision.HIGHEST
    eye = jnp.eye(BLOCK, dtype=jnp.float32)
    inverses, panels, partial = [], [], []
    for k in range(nb):
        lo, up = k * BLOCK, (k + 1) * BLOCK
        factor = lax.linalg.cholesky(system[lo:up, lo:up], symmetrize_input=False)
        inverse = lax.linalg.triangular_solve(factor, eye, left_side=True, lower=True)
        part = jnp.dot(inverse, rhs[lo:up], precision=hi)
        inverses.append(inverse)
        partial.append(part)
        if k + 1 < nb:
            panel = jnp.dot(system[up:, lo:up], inverse.T, precision=hi)
            panels.append(panel)
            trailing = system[up:, up:] - jnp.dot(panel, panel.T, precision=hi)
            system = system.at[up:, up:].set(trailing)
            rhs = rhs.at[up:].add(-jnp.dot(panel, part, precision=hi))
    solved = [None] * nb
    tail = None
    for k in reversed(range(nb)):
        value = partial[k]
        if tail is not None:
            value = value - jnp.dot(tail, panels[k], precision=hi)
        solved[k] = jnp.dot(value, inverses[k], precision=hi)
        tail = solved[k] if tail is None else jnp.concatenate([solved[k], tail])
    return jnp.concatenate(solved)


def sym_matvec(system, v):
    return jnp.sum(system * v[:, None], axis=0)


def certified_cg(system, rhs, lam, steps, tol):
    hi = lax.Precision.HIGHEST
    eye = np.eye(system.shape[0], dtype=bool)
    inv_diag = 1.0 / jnp.sum(jnp.where(eye, system, 0.0), axis=0)
    x = jnp.zeros_like(rhs)
    r = rhs
    z = r * inv_diag
    p = z
    rz = jnp.dot(r, z, precision=hi)
    for _ in range(steps):
        ap = sym_matvec(system, p)
        alpha = rz / jnp.dot(p, ap, precision=hi)
        x = x + alpha * p
        r = r - alpha * ap
        z = r * inv_diag
        rz_next = jnp.dot(r, z, precision=hi)
        p = z + (rz_next / rz) * p
        rz = rz_next
    ax = sym_matvec(system, x)
    resid = rhs - ax
    energy = jnp.dot(x, ax, precision=hi) - lam * jnp.dot(x, x, precision=hi)
    bound = jnp.dot(resid, resid, precision=hi)
    ok = bound <= (tol * tol) * lam * energy
    return x, ok


INTERPRET = False


def cg_kernel(lam, steps, nb, u_ref, b_ref, x_ref, st_ref, pc_ref, lt_ref):
    n = nb * BLOCK
    pairs = upper_pairs(nb)
    for k, (i, j) in enumerate(pairs):
        if i < j:
            lt_ref[k] = jnp.transpose(u_ref[k])

    def matvec(p_row):
        pc_ref[...] = jnp.transpose(jnp.broadcast_to(p_row, (8, n)))
        rows = [jnp.zeros((1, BLOCK), jnp.float32) for _ in range(nb)]
        for k, (i, j) in enumerate(pairs):
            p_i = pc_ref[i * BLOCK : (i + 1) * BLOCK, 0:1]
            rows[j] = rows[j] + jnp.sum(u_ref[k] * p_i, axis=0, keepdims=True)
            if i < j:
                p_j = pc_ref[j * BLOCK : (j + 1) * BLOCK, 0:1]
                rows[i] = rows[i] + jnp.sum(lt_ref[k] * p_j, axis=0, keepdims=True)
        return jnp.concatenate(rows, axis=1) + lam * p_row

    b_row = b_ref[...]
    where = {pair: k for k, pair in enumerate(pairs)}
    eye = lax.broadcasted_iota(jnp.int32, (BLOCK, BLOCK), 0) == lax.broadcasted_iota(
        jnp.int32, (BLOCK, BLOCK), 1
    )
    diag = [
        jnp.sum(jnp.where(eye, u_ref[where[(i, i)]], 0.0), axis=0, keepdims=True)
        for i in range(nb)
    ]
    d_row = 1.0 / (jnp.concatenate(diag, axis=1) + lam)
    z_row = b_row * d_row
    rz = jnp.sum(b_row * z_row, axis=1, keepdims=True)

    def body(_, carry):
        x_row, r_row, p_row, rz = carry
        ap_row = matvec(p_row)
        alpha = rz / jnp.sum(p_row * ap_row, axis=1, keepdims=True)
        x_row = x_row + alpha * p_row
        r_row = r_row - alpha * ap_row
        z_row = r_row * d_row
        rz_next = jnp.sum(r_row * z_row, axis=1, keepdims=True)
        p_row = z_row + (rz_next / rz) * p_row
        return x_row, r_row, p_row, rz_next

    x0 = jnp.zeros((1, n), jnp.float32)
    x_row = lax.fori_loop(0, steps, body, (x0, b_row, z_row, rz))[0]
    ax_row = matvec(x_row)
    resid = b_row - ax_row
    bound = jnp.sum(resid * resid, axis=1, keepdims=True)
    energy = jnp.sum(x_row * ax_row, axis=1, keepdims=True) - lam * jnp.sum(
        x_row * x_row, axis=1, keepdims=True
    )
    x_ref[...] = x_row
    lane = lax.broadcasted_iota(jnp.int32, (1, 128), 1)
    st_ref[...] = jnp.where(lane == 0, bound, jnp.where(lane == 1, energy, 0.0))


def damp_packed(packed, nb, lam):
    where = {pair: k for k, pair in enumerate(upper_pairs(nb))}
    on_diag = np.zeros((len(where), 1, 1), np.float32)
    for i in range(nb):
        on_diag[where[(i, i)]] = 1.0
    eye = np.eye(BLOCK, dtype=np.float32)[None]
    return packed + (lam * on_diag) * eye


def kernel_cg(packed, rhs, lam, steps, tol, nb):
    n = nb * BLOCK
    body = lambda *refs: cg_kernel(lam, steps, nb, *refs)
    x, st = pl.pallas_call(
        body,
        out_shape=(
            jax.ShapeDtypeStruct((1, n), jnp.float32),
            jax.ShapeDtypeStruct((1, 128), jnp.float32),
        ),
        scratch_shapes=[
            pltpu.VMEM((n, 8), jnp.float32),
            pltpu.VMEM(packed.shape, jnp.float32),
        ],
        interpret=INTERPRET,
    )(packed, rhs[None, :])
    ok = st[0, 0] <= (tol * tol) * lam * st[0, 1]
    return x[0], ok


def make_on_device(sizes):
    grp, wx, wz, wc = sizes
    levels = [("wc", wc), ("grp", grp), ("wx", wx), ("wz", wz)]
    levels = [(a, n) for a, n in levels if n > 1]
    n_dev = grp * wx * wz * wc

    def on_device(log_grads, energies):
        walk_axes = WALK_PARTS
        regrouped = lax.all_to_all(
            log_grads, walk_axes, split_axis=1, concat_axis=0, tiled=True
        )
        walk = wx * wz * wc
        group_params = regrouped.shape[1] * walk
        total_params = group_params * grp
        root_walkers = jnp.sqrt(jnp.float32(WALKERS))
        column_mean = jnp.mean(regrouped, axis=0, keepdims=True)
        centred = (regrouped - column_mean) / root_walkers
        local_gram = jnp.dot(centred, centred.T, precision=lax.Precision.HIGHEST)

        nb = WALKERS // BLOCK
        packed = pack_upper(local_gram, nb)
        n_blocks = packed.shape[0]
        flat = packed.reshape(n_blocks * BLOCK, BLOCK)
        chunk = reduce_scatter(flat, levels)
        per_dev = chunk.shape[0]
        energy_row = jnp.zeros((1, BLOCK), jnp.float32)
        energy_row = energy_row.at[0, : energies.shape[0]].set(energies)
        chunk = jnp.concatenate([chunk, energy_row], axis=0)
        gathered = all_gather(chunk, levels[::-1])
        names = [a for a, n in levels]
        gathered = gathered.reshape([n for a, n in levels] + [per_dev + 1, BLOCK])
        whole_packed = gathered[..., :per_dev, :].reshape(n_blocks, BLOCK, BLOCK)
        per_walk = energies.shape[0]
        energy = gathered[..., per_dev, :per_walk]
        if "grp" in names:
            energy = jnp.take(energy, 0, axis=names.index("grp"))
            names.remove("grp")
        order = [names.index(a) for a in WALK_PARTS if a in names]
        all_energy = jnp.transpose(energy, order + [len(names)]).reshape(WALKERS)

        scaled_energy = (all_energy - jnp.mean(all_energy)) / root_walkers
        lam = damping * total_params
        guess, ok = kernel_cg(whole_packed, scaled_energy, lam, CG_STEPS, CG_TOL, nb)
        solved = lax.cond(
            ok,
            lambda a, b, g: g,
            lambda a, b, g: cholesky_solve(
                unpack_upper(damp_packed(a, nb, lam), nb), b, nb
            ),
            whole_packed,
            scaled_energy,
            guess,
        )
        update = jnp.sum(centred * solved[:, None], axis=0)
        return -(total_params / root_walkers) * update

    return on_device


def solution(mesh):
    grp = mesh.shape["grp"]
    walk = mesh.shape["walk"]
    wx, wz, wc = split_walk(walk)
    devices = np.asarray(mesh.devices).reshape(grp, wx, wz, wc)
    fine = Mesh(devices, ("grp",) + WALK_PARTS)
    return jax.shard_map(
        make_on_device((grp, wx, wz, wc)),
        mesh=fine,
        in_specs=(P(WALK_PARTS, "grp"), P(WALK_PARTS)),
        out_specs=P(("grp",) + WALK_PARTS),
        check_vma=False,
    )
```

```python
import jax
import jax.numpy as jnp
import numpy as np
from jax import lax
from jax.experimental import pallas as pl
from jax.experimental.pallas import tpu as pltpu
from jax.sharding import Mesh
from jax.sharding import PartitionSpec as P

WALKERS = 1024
BLOCK = 128
CG_STEPS = 10
CG_TOL = 2e-5


damping = 0.0004

WALK_PARTS = ("wx", "wz", "wc")


def split_walk(walk):
    if walk % 32 == 0 and walk // 32 <= 4:
        return (walk // 32, 16, 2)
    return (1, 1, walk)


def factor_solve(factor, rhs):
    column = rhs[:, None]
    first = lax.linalg.triangular_solve(factor, column, left_side=True, lower=True)
    second = lax.linalg.triangular_solve(
        factor, first, left_side=True, lower=True, transpose_a=True
    )
    return second[:, 0]


def reduce_scatter(x, levels):
    for axis, size in levels:
        rows = x.shape[0]
        parts = x.reshape(size, rows // size, x.shape[1])
        x = lax.all_to_all(parts, axis, 0, 0, tiled=True).sum(0)
    return x


def all_gather(x, levels):
    for axis, size in levels:
        copies = jnp.broadcast_to(x[None], (size,) + x.shape)
        x = lax.all_to_all(copies, axis, 0, 0, tiled=True)
    return x


def upper_pairs(nb):
    return [(i, j) for i in range(nb) for j in range(i, nb)]


def pack_upper(gram, nb):
    blocks = gram.reshape(nb, BLOCK, nb, BLOCK)
    return jnp.stack([blocks[i, :, j, :] for i, j in upper_pairs(nb)])


def unpack_upper(packed, nb):
    where = {pair: k for k, pair in enumerate(upper_pairs(nb))}
    index = np.array(
        [[where[(min(i, j), max(i, j))] for j in range(nb)] for i in range(nb)]
    )
    blocks = packed[index.reshape(-1)].reshape(nb, nb, BLOCK, BLOCK)
    below = np.arange(nb)[:, None] > np.arange(nb)[None, :]
    inner = np.arange(BLOCK)[:, None] > np.arange(BLOCK)[None, :]
    diag = np.eye(nb, dtype=bool)
    mirror = below[:, :, None, None] | (diag[:, :, None, None] & inner[None, None])
    blocks = jnp.where(mirror, jnp.swapaxes(blocks, 2, 3), blocks)
    return jnp.transpose(blocks, (0, 2, 1, 3)).reshape(nb * BLOCK, nb * BLOCK)


def cholesky_solve(system, rhs, nb):
    hi = lax.Precision.HIGHEST
    eye = jnp.eye(BLOCK, dtype=jnp.float32)
    inverses, panels, partial = [], [], []
    for k in range(nb):
        lo, up = k * BLOCK, (k + 1) * BLOCK
        factor = lax.linalg.cholesky(system[lo:up, lo:up], symmetrize_input=False)
        inverse = lax.linalg.triangular_solve(factor, eye, left_side=True, lower=True)
        part = jnp.dot(inverse, rhs[lo:up], precision=hi)
        inverses.append(inverse)
        partial.append(part)
        if k + 1 < nb:
            panel = jnp.dot(system[up:, lo:up], inverse.T, precision=hi)
            panels.append(panel)
            trailing = system[up:, up:] - jnp.dot(panel, panel.T, precision=hi)
            system = system.at[up:, up:].set(trailing)
            rhs = rhs.at[up:].add(-jnp.dot(panel, part, precision=hi))
    solved = [None] * nb
    tail = None
    for k in reversed(range(nb)):
        value = partial[k]
        if tail is not None:
            value = value - jnp.dot(tail, panels[k], precision=hi)
        solved[k] = jnp.dot(value, inverses[k], precision=hi)
        tail = solved[k] if tail is None else jnp.concatenate([solved[k], tail])
    return jnp.concatenate(solved)


def sym_matvec(system, v):
    return jnp.sum(system * v[:, None], axis=0)


def certified_cg(system, rhs, lam, steps, tol):
    hi = lax.Precision.HIGHEST
    eye = np.eye(system.shape[0], dtype=bool)
    inv_diag = 1.0 / jnp.sum(jnp.where(eye, system, 0.0), axis=0)
    x = jnp.zeros_like(rhs)
    r = rhs
    z = r * inv_diag
    p = z
    rz = jnp.dot(r, z, precision=hi)
    for _ in range(steps):
        ap = sym_matvec(system, p)
        alpha = rz / jnp.dot(p, ap, precision=hi)
        x = x + alpha * p
        r = r - alpha * ap
        z = r * inv_diag
        rz_next = jnp.dot(r, z, precision=hi)
        p = z + (rz_next / rz) * p
        rz = rz_next
    ax = sym_matvec(system, x)
    resid = rhs - ax
    energy = jnp.dot(x, ax, precision=hi) - lam * jnp.dot(x, x, precision=hi)
    bound = jnp.dot(resid, resid, precision=hi)
    ok = bound <= (tol * tol) * lam * energy
    return x, ok


INTERPRET = False


def cg_kernel(lam, steps, nb, u_ref, b_ref, x_ref, st_ref, pc_ref, lt_ref):
    n = nb * BLOCK
    pairs = upper_pairs(nb)
    for k, (i, j) in enumerate(pairs):
        if i < j:
            lt_ref[k] = jnp.transpose(u_ref[k])

    def matvec(p_row):
        pc_ref[...] = jnp.transpose(jnp.broadcast_to(p_row, (8, n)))
        rows = [jnp.zeros((1, BLOCK), jnp.float32) for _ in range(nb)]
        for k, (i, j) in enumerate(pairs):
            p_i = pc_ref[i * BLOCK : (i + 1) * BLOCK, 0:1]
            rows[j] = rows[j] + jnp.sum(u_ref[k] * p_i, axis=0, keepdims=True)
            if i < j:
                p_j = pc_ref[j * BLOCK : (j + 1) * BLOCK, 0:1]
                rows[i] = rows[i] + jnp.sum(lt_ref[k] * p_j, axis=0, keepdims=True)
        return jnp.concatenate(rows, axis=1) + lam * p_row

    raw = b_ref[...]
    b_row = (raw - jnp.sum(raw, axis=1, keepdims=True) / n) / jnp.sqrt(jnp.float32(n))
    where = {pair: k for k, pair in enumerate(pairs)}
    eye = lax.broadcasted_iota(jnp.int32, (BLOCK, BLOCK), 0) == lax.broadcasted_iota(
        jnp.int32, (BLOCK, BLOCK), 1
    )
    diag = [
        jnp.sum(jnp.where(eye, u_ref[where[(i, i)]], 0.0), axis=0, keepdims=True)
        for i in range(nb)
    ]
    d_row = 1.0 / (jnp.concatenate(diag, axis=1) + lam)
    z_row = b_row * d_row
    rz = jnp.sum(b_row * z_row, axis=1, keepdims=True)

    def body(_, carry):
        x_row, r_row, p_row, rz = carry
        ap_row = matvec(p_row)
        alpha = rz / jnp.sum(p_row * ap_row, axis=1, keepdims=True)
        x_row = x_row + alpha * p_row
        r_row = r_row - alpha * ap_row
        z_row = r_row * d_row
        rz_next = jnp.sum(r_row * z_row, axis=1, keepdims=True)
        p_row = z_row + (rz_next / rz) * p_row
        return x_row, r_row, p_row, rz_next

    x0 = jnp.zeros((1, n), jnp.float32)
    x_row = lax.fori_loop(0, steps, body, (x0, b_row, z_row, rz))[0]
    ax_row = matvec(x_row)
    resid = b_row - ax_row
    bound = jnp.sum(resid * resid, axis=1, keepdims=True)
    energy = jnp.sum(x_row * ax_row, axis=1, keepdims=True) - lam * jnp.sum(
        x_row * x_row, axis=1, keepdims=True
    )
    x_ref[...] = x_row
    lane = lax.broadcasted_iota(jnp.int32, (1, 128), 1)
    st_ref[...] = jnp.where(lane == 0, bound, jnp.where(lane == 1, energy, 0.0))


def damp_packed(packed, nb, lam):
    where = {pair: k for k, pair in enumerate(upper_pairs(nb))}
    on_diag = np.zeros((len(where), 1, 1), np.float32)
    for i in range(nb):
        on_diag[where[(i, i)]] = 1.0
    eye = np.eye(BLOCK, dtype=np.float32)[None]
    return packed + (lam * on_diag) * eye


def kernel_cg(packed, rhs, lam, steps, tol, nb):
    n = nb * BLOCK
    body = lambda *refs: cg_kernel(lam, steps, nb, *refs)
    x, st = pl.pallas_call(
        body,
        out_shape=(
            jax.ShapeDtypeStruct((1, n), jnp.float32),
            jax.ShapeDtypeStruct((1, 128), jnp.float32),
        ),
        scratch_shapes=[
            pltpu.VMEM((n, 8), jnp.float32),
            pltpu.VMEM(packed.shape, jnp.float32),
        ],
        interpret=INTERPRET,
    )(packed, rhs[None, :])
    ok = st[0, 0] <= (tol * tol) * lam * st[0, 1]
    return x[0], ok


def make_on_device(sizes):
    grp, wx, wz, wc = sizes
    levels = [("wc", wc), ("grp", grp), ("wx", wx), ("wz", wz)]
    levels = [(a, n) for a, n in levels if n > 1]
    n_dev = grp * wx * wz * wc

    def on_device(log_grads, energies):
        walk_axes = WALK_PARTS
        regrouped = lax.all_to_all(
            log_grads, walk_axes, split_axis=1, concat_axis=0, tiled=True
        )
        walk = wx * wz * wc
        group_params = regrouped.shape[1] * walk
        total_params = group_params * grp
        root_walkers = jnp.sqrt(jnp.float32(WALKERS))
        column_mean = jnp.mean(regrouped, axis=0, keepdims=True)
        centred = (regrouped - column_mean) / root_walkers
        local_gram = jnp.dot(centred, centred.T, precision=lax.Precision.HIGHEST)

        nb = WALKERS // BLOCK
        packed = pack_upper(local_gram, nb)
        n_blocks = packed.shape[0]
        flat = packed.reshape(n_blocks * BLOCK, BLOCK)
        chunk = reduce_scatter(flat, levels)
        per_dev = chunk.shape[0]
        energy_row = jnp.zeros((1, BLOCK), jnp.float32)
        energy_row = energy_row.at[0, : energies.shape[0]].set(energies)
        chunk = jnp.concatenate([chunk, energy_row], axis=0)
        gathered = all_gather(chunk, levels[::-1])
        names = [a for a, n in levels]
        gathered = gathered.reshape([n for a, n in levels] + [per_dev + 1, BLOCK])
        whole_packed = gathered[..., :per_dev, :].reshape(n_blocks, BLOCK, BLOCK)
        per_walk = energies.shape[0]
        energy = gathered[..., per_dev, :per_walk]
        if "grp" in names:
            energy = jnp.take(energy, 0, axis=names.index("grp"))
            names.remove("grp")
        order = [names.index(a) for a in WALK_PARTS if a in names]
        all_energy = jnp.transpose(energy, order + [len(names)]).reshape(WALKERS)

        lam = damping * total_params
        guess, ok = kernel_cg(whole_packed, all_energy, lam, CG_STEPS, CG_TOL, nb)
        solved = lax.cond(
            ok,
            lambda a, b, g: g,
            lambda a, b, g: cholesky_solve(
                unpack_upper(damp_packed(a, nb, lam), nb),
                (b - jnp.mean(b)) / root_walkers,
                nb,
            ),
            whole_packed,
            all_energy,
            guess,
        )
        update = jnp.sum(centred * solved[:, None], axis=0)
        return -(total_params / root_walkers) * update

    return on_device


def solution(mesh):
    grp = mesh.shape["grp"]
    walk = mesh.shape["walk"]
    wx, wz, wc = split_walk(walk)
    devices = np.asarray(mesh.devices).reshape(grp, wx, wz, wc)
    fine = Mesh(devices, ("grp",) + WALK_PARTS)
    return jax.shard_map(
        make_on_device((grp, wx, wz, wc)),
        mesh=fine,
        in_specs=(P(WALK_PARTS, "grp"), P(WALK_PARTS)),
        out_specs=P(("grp",) + WALK_PARTS),
        check_vma=False,
    )
```

```python
import jax
import jax.numpy as jnp
import numpy as np
from jax import lax
from jax.experimental import pallas as pl
from jax.experimental.pallas import tpu as pltpu
from jax.sharding import Mesh
from jax.sharding import PartitionSpec as P

WALKERS = 1024
BLOCK = 128
CG_STEPS = 10
CG_TOL = 2e-5


damping = 0.0004

WALK_PARTS = ("wx", "wz", "wc")


def split_walk(walk):
    if walk % 32 == 0 and walk // 32 <= 4:
        return (walk // 32, 16, 2)
    return (1, 1, walk)


def factor_solve(factor, rhs):
    column = rhs[:, None]
    first = lax.linalg.triangular_solve(factor, column, left_side=True, lower=True)
    second = lax.linalg.triangular_solve(
        factor, first, left_side=True, lower=True, transpose_a=True
    )
    return second[:, 0]


def reduce_scatter(x, levels):
    for axis, size in levels:
        rows = x.shape[0]
        parts = x.reshape(size, rows // size, x.shape[1])
        x = lax.all_to_all(parts, axis, 0, 0, tiled=True).sum(0)
    return x


def all_gather(x, levels):
    for axis, size in levels:
        copies = jnp.broadcast_to(x[None], (size,) + x.shape)
        x = lax.all_to_all(copies, axis, 0, 0, tiled=True)
    return x


def upper_pairs(nb):
    return [(i, j) for i in range(nb) for j in range(i, nb)]


def pack_upper(gram, nb):
    blocks = gram.reshape(nb, BLOCK, nb, BLOCK)
    return jnp.stack([blocks[i, :, j, :] for i, j in upper_pairs(nb)])


def unpack_upper(packed, nb):
    where = {pair: k for k, pair in enumerate(upper_pairs(nb))}
    index = np.array(
        [[where[(min(i, j), max(i, j))] for j in range(nb)] for i in range(nb)]
    )
    blocks = packed[index.reshape(-1)].reshape(nb, nb, BLOCK, BLOCK)
    below = np.arange(nb)[:, None] > np.arange(nb)[None, :]
    inner = np.arange(BLOCK)[:, None] > np.arange(BLOCK)[None, :]
    diag = np.eye(nb, dtype=bool)
    mirror = below[:, :, None, None] | (diag[:, :, None, None] & inner[None, None])
    blocks = jnp.where(mirror, jnp.swapaxes(blocks, 2, 3), blocks)
    return jnp.transpose(blocks, (0, 2, 1, 3)).reshape(nb * BLOCK, nb * BLOCK)


def cholesky_solve(system, rhs, nb):
    hi = lax.Precision.HIGHEST
    eye = jnp.eye(BLOCK, dtype=jnp.float32)
    inverses, panels, partial = [], [], []
    for k in range(nb):
        lo, up = k * BLOCK, (k + 1) * BLOCK
        factor = lax.linalg.cholesky(system[lo:up, lo:up], symmetrize_input=False)
        inverse = lax.linalg.triangular_solve(factor, eye, left_side=True, lower=True)
        part = jnp.dot(inverse, rhs[lo:up], precision=hi)
        inverses.append(inverse)
        partial.append(part)
        if k + 1 < nb:
            panel = jnp.dot(system[up:, lo:up], inverse.T, precision=hi)
            panels.append(panel)
            trailing = system[up:, up:] - jnp.dot(panel, panel.T, precision=hi)
            system = system.at[up:, up:].set(trailing)
            rhs = rhs.at[up:].add(-jnp.dot(panel, part, precision=hi))
    solved = [None] * nb
    tail = None
    for k in reversed(range(nb)):
        value = partial[k]
        if tail is not None:
            value = value - jnp.dot(tail, panels[k], precision=hi)
        solved[k] = jnp.dot(value, inverses[k], precision=hi)
        tail = solved[k] if tail is None else jnp.concatenate([solved[k], tail])
    return jnp.concatenate(solved)


def sym_matvec(system, v):
    return jnp.sum(system * v[:, None], axis=0)


def certified_cg(system, rhs, lam, steps, tol):
    hi = lax.Precision.HIGHEST
    eye = np.eye(system.shape[0], dtype=bool)
    inv_diag = 1.0 / jnp.sum(jnp.where(eye, system, 0.0), axis=0)
    x = jnp.zeros_like(rhs)
    r = rhs
    z = r * inv_diag
    p = z
    rz = jnp.dot(r, z, precision=hi)
    for _ in range(steps):
        ap = sym_matvec(system, p)
        alpha = rz / jnp.dot(p, ap, precision=hi)
        x = x + alpha * p
        r = r - alpha * ap
        z = r * inv_diag
        rz_next = jnp.dot(r, z, precision=hi)
        p = z + (rz_next / rz) * p
        rz = rz_next
    ax = sym_matvec(system, x)
    resid = rhs - ax
    energy = jnp.dot(x, ax, precision=hi) - lam * jnp.dot(x, x, precision=hi)
    bound = jnp.dot(resid, resid, precision=hi)
    ok = bound <= (tol * tol) * lam * energy
    return x, ok


INTERPRET = False


def cg_kernel(lam, steps, nb, u_ref, b_ref, x_ref, st_ref, pc_ref, lt_ref):
    n = nb * BLOCK
    pairs = upper_pairs(nb)
    for k, (i, j) in enumerate(pairs):
        if i < j:
            lt_ref[k] = jnp.transpose(u_ref[k])

    def matvec(p_row):
        pc_ref[...] = jnp.transpose(jnp.broadcast_to(p_row, (8, n)))
        rows = [jnp.zeros((1, BLOCK), jnp.float32) for _ in range(nb)]
        for k, (i, j) in enumerate(pairs):
            p_i = pc_ref[i * BLOCK : (i + 1) * BLOCK, 0:1]
            rows[j] = rows[j] + jnp.sum(u_ref[k] * p_i, axis=0, keepdims=True)
            if i < j:
                p_j = pc_ref[j * BLOCK : (j + 1) * BLOCK, 0:1]
                rows[i] = rows[i] + jnp.sum(lt_ref[k] * p_j, axis=0, keepdims=True)
        return jnp.concatenate(rows, axis=1) + lam * p_row

    raw = b_ref[...]
    b_row = (raw - jnp.sum(raw, axis=1, keepdims=True) / n) / jnp.sqrt(jnp.float32(n))
    where = {pair: k for k, pair in enumerate(pairs)}
    eye = lax.broadcasted_iota(jnp.int32, (BLOCK, BLOCK), 0) == lax.broadcasted_iota(
        jnp.int32, (BLOCK, BLOCK), 1
    )
    diag = [
        jnp.sum(jnp.where(eye, u_ref[where[(i, i)]], 0.0), axis=0, keepdims=True)
        for i in range(nb)
    ]
    d_row = 1.0 / (jnp.concatenate(diag, axis=1) + lam)
    z_row = b_row * d_row
    rz = jnp.sum(b_row * z_row, axis=1, keepdims=True)

    def body(_, carry):
        x_row, r_row, p_row, rz = carry
        ap_row = matvec(p_row)
        alpha = rz / jnp.sum(p_row * ap_row, axis=1, keepdims=True)
        x_row = x_row + alpha * p_row
        r_row = r_row - alpha * ap_row
        z_row = r_row * d_row
        rz_next = jnp.sum(r_row * z_row, axis=1, keepdims=True)
        p_row = z_row + (rz_next / rz) * p_row
        return x_row, r_row, p_row, rz_next

    x0 = jnp.zeros((1, n), jnp.float32)
    x_row = lax.fori_loop(0, steps, body, (x0, b_row, z_row, rz))[0]
    ax_row = matvec(x_row)
    resid = b_row - ax_row
    bound = jnp.sum(resid * resid, axis=1, keepdims=True)
    energy = jnp.sum(x_row * ax_row, axis=1, keepdims=True) - lam * jnp.sum(
        x_row * x_row, axis=1, keepdims=True
    )
    x_ref[...] = x_row
    lane = lax.broadcasted_iota(jnp.int32, (1, 128), 1)
    st_ref[...] = jnp.where(lane == 0, bound, jnp.where(lane == 1, energy, 0.0))


def damp_packed(packed, nb, lam):
    where = {pair: k for k, pair in enumerate(upper_pairs(nb))}
    on_diag = np.zeros((len(where), 1, 1), np.float32)
    for i in range(nb):
        on_diag[where[(i, i)]] = 1.0
    eye = np.eye(BLOCK, dtype=np.float32)[None]
    return packed + (lam * on_diag) * eye


def kernel_cg(packed, rhs, lam, steps, tol, nb):
    n = nb * BLOCK
    body = lambda *refs: cg_kernel(lam, steps, nb, *refs)
    x, st = pl.pallas_call(
        body,
        out_shape=(
            jax.ShapeDtypeStruct((1, n), jnp.float32),
            jax.ShapeDtypeStruct((1, 128), jnp.float32),
        ),
        scratch_shapes=[
            pltpu.VMEM((n, 8), jnp.float32),
            pltpu.VMEM(packed.shape, jnp.float32),
        ],
        interpret=INTERPRET,
    )(packed, rhs[None, :])
    ok = st[0, 0] <= (tol * tol) * lam * st[0, 1]
    return x[0], ok


def make_on_device(sizes):
    grp, wx, wz, wc = sizes
    levels = [("wc", wc), ("grp", grp), ("wx", wx), ("wz", wz)]
    levels = [(a, n) for a, n in levels if n > 1]
    n_dev = grp * wx * wz * wc

    def on_device(log_grads, energies):
        walk_axes = WALK_PARTS
        regrouped = lax.all_to_all(
            log_grads, walk_axes, split_axis=1, concat_axis=0, tiled=True
        )
        walk = wx * wz * wc
        group_params = regrouped.shape[1] * walk
        total_params = group_params * grp
        root_walkers = jnp.sqrt(jnp.float32(WALKERS))
        column_mean = jnp.mean(regrouped, axis=0, keepdims=True)
        centred = (regrouped - column_mean) / root_walkers
        local_gram = jnp.dot(centred, centred.T, precision=lax.Precision.HIGHEST)

        nb = WALKERS // BLOCK
        packed = pack_upper(local_gram, nb)
        n_blocks = packed.shape[0]
        flat = packed.reshape(n_blocks * BLOCK, BLOCK)
        chunk = reduce_scatter(flat, levels)
        per_dev = chunk.shape[0]
        energy_row = jnp.zeros((1, BLOCK), jnp.float32)
        energy_row = energy_row.at[0, : energies.shape[0]].set(energies)
        chunk = jnp.concatenate([chunk, energy_row], axis=0)
        gathered = all_gather(chunk, levels[::-1])
        names = [a for a, n in levels]
        gathered = gathered.reshape([n for a, n in levels] + [per_dev + 1, BLOCK])
        whole_packed = gathered[..., :per_dev, :].reshape(n_blocks, BLOCK, BLOCK)
        per_walk = energies.shape[0]
        energy = gathered[..., per_dev, :per_walk]
        if "grp" in names:
            energy = jnp.take(energy, 0, axis=names.index("grp"))
            names.remove("grp")
        order = [names.index(a) for a in WALK_PARTS if a in names]
        all_energy = jnp.transpose(energy, order + [len(names)]).reshape(WALKERS)

        lam = damping * total_params
        guess, ok = kernel_cg(whole_packed, all_energy, lam, CG_STEPS, CG_TOL, nb)
        solved = lax.cond(
            ok,
            lambda a, b, g: g,
            lambda a, b, g: cholesky_solve(
                unpack_upper(damp_packed(a, nb, lam), nb),
                (b - jnp.mean(b)) / root_walkers,
                nb,
            ),
            whole_packed,
            all_energy,
            guess,
        )
        scaled = -(total_params / root_walkers) * solved
        return jnp.sum(centred * scaled[:, None], axis=0)

    return on_device


def solution(mesh):
    grp = mesh.shape["grp"]
    walk = mesh.shape["walk"]
    wx, wz, wc = split_walk(walk)
    devices = np.asarray(mesh.devices).reshape(grp, wx, wz, wc)
    fine = Mesh(devices, ("grp",) + WALK_PARTS)
    return jax.shard_map(
        make_on_device((grp, wx, wz, wc)),
        mesh=fine,
        in_specs=(P(WALK_PARTS, "grp"), P(WALK_PARTS)),
        out_specs=P(("grp",) + WALK_PARTS),
        check_vma=False,
    )
```
